1024 devices in a mesh: leaf: 64 (over x, y), sub: 16 (over z, core).
Axes of the slice: x: 8, y: 8, z: 8, core: 2. Of those that a mesh axis runs over, the one named last changes fastest.
Arguments:
- p_dirs: float32 [16, 2097152], P(None, ('leaf', 'sub')), may hold values from -6 to 6
- resid: float32 [16, 2097152], P(None, ('leaf', 'sub')), may hold values from -6 to 6
- perm: int32 [1024, 2048], P(('leaf', 'sub')), may hold values from 0 to 2047, each once within a row
- col_basis: bfloat16 [32768, 64, 32], P(('leaf', 'sub')), may hold values from -0.75 to 0.75
- row_basis: bfloat16 [32768, 64, 32], P(('leaf', 'sub')), may hold values from -0.25 to 0.25
- near_blocks: bfloat16 [32768, 6, 4096], P(('leaf', 'sub')), may hold values from -0.3125 to 0.3125
- near_scale: float32 [32768, 6], P(('leaf', 'sub')), may hold values from 0.3 to 3
- near_index: int32 [32768, 6], P(('leaf', 'sub')), may hold values from 0 to 96, as said below
- far_blocks: bfloat16 [32768, 6, 1024], P(('leaf', 'sub')), may hold values from -0.4375 to 0.4375
- far_scale: float32 [32768, 6], P(('leaf', 'sub')), may hold values from 0.3 to 3
- far_index: int32 [32768, 6], P(('leaf', 'sub')), may hold values from 0 to 96, as said below
- loc_col: bfloat16 [1024, 62, 32, 32], P(('leaf', 'sub')), may hold values from -0.084852814 to 0.804852814
- loc_row: bfloat16 [1024, 62, 32, 32], P(('leaf', 'sub')), may hold values from -0.11844038584874671 to 1.1284404
- up_col: float32 [2, 32, 32], replicated, may hold values from -0.084852814 to 0.804852814
- up_row: float32 [2, 32, 32], replicated, may hold values from -0.11844038584874671 to 1.1284404
- up_cpl: float32 [2, 32, 32], replicated, may hold values from -1 to 1
Outputs:
- p_image: float32 [16, 2097152], P(None, ('leaf', 'sub'))
- r_image: float32 [16, 2097152], P(None, ('leaf', 'sub'))
The draws below stay inside these ranges and needn't reach their ends.
Inputs may be any that keep to these rules, and one draw needn't show every extreme that they name: `perm`: each row names every number once. `near_index`: slot 0 of leaf g's list names the leaf itself, 32 + g mod 32. Live slots come first; every list has two or more, and the rest hold 96. `far_index`: live slots come first; every list has two or more, and the rest hold 96.
All inputs are finite; a program needn't handle non-finite values.
Results may differ from the reference program's by a relative error of at most 0.0039.
Values may be sent and summed in bfloat16 or wider, within the bound.
No kernel may reach another device: no remote copies, remote signals or barrier semaphores. Data moves between devices by JAX's collectives and lax.ppermute only.
A program may use at most 128 MiB of HBM per device.

```python
import math
import jax
import jax.numpy as jnp
from jax import lax

LEAF = 64
RANK = 32
RHS = 16
NEAR = 6
FAR = 6
LEAVES_DEV = 32
PTS_DEV = 2048
LEAVES = 32768
POINTS = 2097152
N_LEAF = 64
N_SUB = 16
DEVICES = 1024


def index_lists(key, slot_total, self_first):
    split_keys = jax.random.split(key, 2)
    leaf_ids = jnp.arange(LEAVES, dtype=jnp.int32)
    within = leaf_ids % LEAVES_DEV
    offsets = jax.random.randint(split_keys[0], (LEAVES, slot_total), -LEAVES_DEV, LEAVES_DEV + 1, dtype=jnp.int32)
    slot_ids = jnp.arange(slot_total, dtype=jnp.int32)[None, :]
    target = LEAVES_DEV + within[:, None] + offsets
    if self_first:
        target = jnp.where(slot_ids == 0, LEAVES_DEV + within[:, None], target)
    target = jnp.where((within[:, None] == 0) & (slot_ids == 1), 0, target)
    live_count = jax.random.randint(split_keys[1], (LEAVES, 1), 2, slot_total + 1, dtype=jnp.int32)
    live_count = jnp.where(within[:, None] == LEAVES_DEV - 1, jnp.minimum(live_count, slot_total - 1), live_count)
    return jnp.where(slot_ids >= live_count, 3 * LEAVES_DEV, target).astype(jnp.int32)


def draw_near_index(key, part):
    return index_lists(jax.random.fold_in(key, 11), NEAR, True)


def draw_far_index(key, part):
    return index_lists(jax.random.fold_in(key, 23), FAR, False)


def transfer_law(key, out_shape, factor):
    noise_part = jnp.clip(jax.random.normal(key, out_shape, jnp.float32), -3.0, 3.0)
    row_ids = jnp.arange(RANK)[:, None]
    col_ids = jnp.arange(RANK)[None, :]
    unit_diag = jnp.where(row_ids == col_ids, 1.0, 0.0).astype(jnp.float32)
    return (unit_diag + 0.22 / math.sqrt(RANK) * noise_part) * factor


def draw_up_col(key, part):
    return transfer_law(jax.random.fold_in(key, 31), (2, RANK, RANK), 1.0 / math.sqrt(2.0))


def draw_up_row(key, part):
    return transfer_law(jax.random.fold_in(key, 37), (2, RANK, RANK), 1.0)


def draw_loc_col(key, part):
    device_total = LEAVES // LEAVES_DEV
    return transfer_law(jax.random.fold_in(key, 41), (device_total, 2 * LEAVES_DEV - 2, RANK, RANK), 1.0 / math.sqrt(2.0)).astype(jnp.bfloat16)


def draw_loc_row(key, part):
    device_total = LEAVES // LEAVES_DEV
    return transfer_law(jax.random.fold_in(key, 43), (device_total, 2 * LEAVES_DEV - 2, RANK, RANK), 1.0).astype(jnp.bfloat16)


def shard_levels(rng, dims, cuts, smallest, top_value):
    def one(axis_at, shards_of):
        draws = jax.random.uniform(jax.random.fold_in(jax.random.fold_in(rng, 6), axis_at), (shards_of,), jnp.float32, smallest / len(cuts), top_value / len(cuts))
        return jnp.repeat(jnp.exp(draws), dims[axis_at] // shards_of).reshape((-1,) + (1,) * (len(dims) - axis_at - 1))

    factor_of = one(*cuts[0])
    for cut in cuts[1:]:
        factor_of = factor_of * one(*cut)
    return factor_of


def centred(key, shape, width, most, cuts=(), kind=jnp.bfloat16):
    factor_of = shard_levels(key, shape, cuts, -0.22, 0.18) if cuts else 1.0
    entries = jax.random.normal(key, shape, jnp.float32) * width * factor_of
    return jnp.minimum(jnp.maximum(entries, -most), most).astype(kind)


def setup_inputs(seed: int = 0) -> dict:
    key_list = jax.random.split(jax.random.key(seed), 17)
    return {
        "p_dirs": centred(key_list[0], (RHS, POINTS), 1.0, 6.0, ((1, 1024),), jnp.float32),
        "resid": centred(key_list[1], (RHS, POINTS), 1.0, 6.0, ((1, 1024),), jnp.float32),
        "perm": jax.vmap(lambda own: jax.random.permutation(own, PTS_DEV))(jax.random.split(key_list[2], DEVICES)).reshape((DEVICES, PTS_DEV)).astype(jnp.int32),
        "col_basis": centred(key_list[3], (LEAVES, LEAF, RANK), LEAF ** -0.5, 0.75, ((0, 1024),)),
        "row_basis": centred(key_list[4], (LEAVES, LEAF, RANK), (16 * RANK) ** -0.5, 0.25, ((0, 1024),)),
        "near_blocks": centred(key_list[5], (LEAVES, NEAR, LEAF * LEAF), (LEAF * NEAR) ** -0.5, 0.3125, ((0, 1024),)),
        "near_scale": jnp.clip(jnp.exp(math.log(3.0) - 2.3025851 * jax.random.uniform(key_list[6], (LEAVES, NEAR), jnp.float32) ** shard_levels(key_list[6], (LEAVES, NEAR), ((0, 1024),), -0.2, 0.2)), 0.3, 3.0),
        "near_index": draw_near_index(jax.random.fold_in(key_list[16], 71), 0),
        "far_blocks": centred(key_list[8], (LEAVES, FAR, RANK * RANK), (RANK * FAR) ** -0.5, 0.4375, ((0, 1024),)),
        "far_scale": jnp.clip(jnp.exp(math.log(3.0) - 2.3025851 * jax.random.uniform(key_list[9], (LEAVES, FAR), jnp.float32) ** shard_levels(key_list[9], (LEAVES, FAR), ((0, 1024),), -0.2, 0.2)), 0.3, 3.0),
        "far_index": draw_far_index(jax.random.fold_in(key_list[16], 71), 0),
        "loc_col": draw_loc_col(jax.random.fold_in(key_list[16], 71), 0),
        "loc_row": draw_loc_row(jax.random.fold_in(key_list[16], 71), 0),
        "up_col": draw_up_col(jax.random.fold_in(key_list[16], 71), 0),
        "up_row": draw_up_row(jax.random.fold_in(key_list[16], 71), 0),
        "up_cpl": centred(key_list[15], (2, RANK, RANK), RANK ** -0.5, 1.0, (), jnp.float32),
    }


best_precision = lax.Precision.HIGHEST


def apply_up(matrix, coeffs):
    return jnp.einsum('...ab,...ac->...bc', matrix, coeffs, precision=best_precision)


def apply_down(matrix, coeffs):
    return jnp.einsum('...ab,...bc->...ac', matrix, coeffs, precision=best_precision)


def side_window(leaf_grid, concat_axis):
    zero_rim = jnp.zeros_like(leaf_grid[:, :1])
    before = jnp.concatenate([zero_rim, leaf_grid[:, :-1]], axis=1)
    after_rim = jnp.concatenate([leaf_grid[:, 1:], zero_rim], axis=1)
    return jnp.concatenate([before, leaf_grid, after_rim], axis=concat_axis)


def finish_device(pieces):
    local_field, coeff_win, x_win, far_blk, far_wt, far_idx, near_blk, near_wt, near_idx, row_blk = pieces
    width_all = coeff_win.shape[0]
    far_live = far_idx < width_all
    far_safe = jnp.minimum(far_idx, width_all - 1)
    picked = coeff_win[far_safe].astype(jnp.float32)
    far_terms = jnp.einsum('lkab,lkbc->lkac', far_blk.astype(jnp.float32), picked, precision=best_precision)
    far_weight = jnp.where(far_live, far_wt, jnp.zeros_like(far_wt))
    leaf_field = local_field + jnp.einsum('lkac,lk->lac', far_terms, far_weight, precision=best_precision)
    field_round = lax.optimization_barrier(leaf_field.astype(jnp.bfloat16))
    far_out = jnp.einsum('lpk,lkc->clp', row_blk.astype(jnp.float32), field_round.astype(jnp.float32), precision=best_precision)
    near_live = near_idx < width_all
    near_safe = jnp.minimum(near_idx, width_all - 1)
    near_pick = x_win[:, near_safe].astype(jnp.float32)
    near_terms = jnp.einsum('lkpq,clkq->clkp', near_blk.astype(jnp.float32), near_pick, precision=best_precision)
    near_weight = jnp.where(near_live, near_wt, jnp.zeros_like(near_wt))
    near_sum = jnp.einsum('clkp,lk->clp', near_terms, near_weight, precision=best_precision)
    image = far_out + near_sum
    return image.reshape(image.shape[0], image.shape[1] * image.shape[2])


def kernel_image(vectors, perm, col_basis, row_basis, near_blocks, near_scale, near_index, far_blocks, far_scale, far_index, loc_col, loc_row, up_col, up_row, up_cpl):
    devices = N_LEAF * N_SUB
    leaves_dev = col_basis.shape[0] // devices
    leaf_size = col_basis.shape[1]
    rank_width = col_basis.shape[2]
    columns = vectors.shape[0]
    pts_dev = leaves_dev * leaf_size
    per_device = vectors.reshape(columns, devices, pts_dev).transpose(1, 0, 2)
    ordered = jax.vmap(lambda block_rows, order_row: block_rows[:, order_row])(per_device, perm)
    ordered = lax.optimization_barrier(ordered.astype(jnp.bfloat16))
    leaf_blocks = ordered.reshape(devices, columns, leaves_dev, leaf_size)
    x_window = side_window(leaf_blocks.reshape(N_LEAF, N_SUB, columns, leaves_dev, leaf_size), 3)
    x_window = x_window.reshape(devices, columns, 3 * leaves_dev, leaf_size)
    basis_dev = col_basis.reshape(devices, leaves_dev, leaf_size, rank_width)
    leaf_coeff = jnp.einsum('dclp,dlpk->dlkc', leaf_blocks.astype(jnp.float32), basis_dev.astype(jnp.float32), precision=best_precision)
    leaf_round = lax.optimization_barrier(leaf_coeff.astype(jnp.bfloat16))
    c_window = side_window(leaf_round.reshape(N_LEAF, N_SUB, leaves_dev, rank_width, columns), 2)
    c_window = c_window.reshape(devices, 3 * leaves_dev, rank_width, columns)
    col_local = loc_col.astype(jnp.float32)
    row_local = loc_row.astype(jnp.float32)
    current = leaf_coeff
    offsets = []
    start_at = 0
    while current.shape[1] > 1:
        node_count = current.shape[1]
        moved_up = apply_up(col_local[:, start_at:start_at + node_count], current)
        paired = moved_up.reshape(devices, node_count // 2, 2, rank_width, columns)
        current = paired[:, :, 0] + paired[:, :, 1]
        offsets.append(start_at)
        start_at = start_at + node_count
    upper_now = current[:, 0]
    up_levels = devices.bit_length() - 1
    levels = []
    for level_num in range(up_levels):
        levels.append(upper_now)
        if level_num + 1 < up_levels:
            paired = upper_now.reshape(-1, 2, rank_width, columns)
            upper_now = apply_up(up_col[0], paired[:, 0]) + apply_up(up_col[1], paired[:, 1])
    field_now = jnp.zeros((1, rank_width, columns), jnp.float32)
    for level_num in reversed(range(up_levels)):
        level_nodes = levels[level_num]
        node_count = level_nodes.shape[0]
        paired = level_nodes.reshape(node_count // 2, 2, rank_width, columns)
        sibling = jnp.stack([paired[:, 1], paired[:, 0]], axis=1)
        parent = field_now[:, None]
        field_now = (apply_down(up_row, parent) + apply_down(up_cpl, sibling)).reshape(node_count, rank_width, columns)
    local_field = field_now[:, None]
    for start_at in reversed(offsets):
        node_count = local_field.shape[1] * 2
        local_field = apply_down(row_local[:, start_at:start_at + node_count], jnp.repeat(local_field, 2, axis=1))
    far_count = far_blocks.shape[1]
    near_count = near_blocks.shape[1]
    pieces = (
        local_field,
        c_window,
        x_window,
        far_blocks.reshape(devices, leaves_dev, far_count, rank_width, rank_width),
        far_scale.reshape(devices, leaves_dev, far_count),
        far_index.reshape(devices, leaves_dev, far_count),
        near_blocks.reshape(devices, leaves_dev, near_count, leaf_size, leaf_size),
        near_scale.reshape(devices, leaves_dev, near_count),
        near_index.reshape(devices, leaves_dev, near_count),
        row_basis.reshape(devices, leaves_dev, leaf_size, rank_width),
    )
    tree_image = lax.map(finish_device, pieces)
    placed = jax.vmap(lambda block_rows, order_row: jnp.zeros_like(block_rows).at[:, order_row].set(block_rows))(tree_image, perm)
    return placed.transpose(1, 0, 2).reshape(columns, devices * pts_dev)


def reference(p_dirs, resid, perm, col_basis, row_basis, near_blocks, near_scale, near_index, far_blocks, far_scale, far_index, loc_col, loc_row, up_col, up_row, up_cpl):
    p_image = kernel_image(p_dirs, perm, col_basis, row_basis, near_blocks, near_scale, near_index, far_blocks, far_scale, far_index, loc_col, loc_row, up_col, up_row, up_cpl)
    r_image = kernel_image(resid, perm, col_basis, row_basis, near_blocks, near_scale, near_index, far_blocks, far_scale, far_index, loc_col, loc_row, up_col, up_row, up_cpl)
    return (p_image, r_image)
```

```python
import jax
import jax.numpy as jnp
from jax import lax
from jax.sharding import PartitionSpec as P

best_precision = lax.Precision.HIGHEST


def extended(block, axis, dim):
    count = lax.axis_size(axis)
    forward = [(i, i + 1) for i in range(count - 1)]
    backward = [(target, source) for source, target in forward]
    low = lax.ppermute(block, axis, forward)
    high = lax.ppermute(block, axis, backward)
    return jnp.concatenate([low, block, high], axis=dim)


def apply_up(matrix, coeffs):
    return jnp.einsum("...ab,...ac->...bc", matrix, coeffs, precision=best_precision)


def apply_down(matrix, coeffs):
    return jnp.einsum("...ab,...bc->...ac", matrix, coeffs, precision=best_precision)


def shards(
    p_dirs,
    resid,
    perm,
    col_basis,
    row_basis,
    near_blocks,
    near_scale,
    near_index,
    far_blocks,
    far_scale,
    far_index,
    loc_col,
    loc_row,
    up_col,
    up_row,
    up_cpl,
):
    leaves_dev, leaf_size, rank_width = col_basis.shape
    near_square = near_blocks.reshape(leaves_dev, near_blocks.shape[1], leaf_size, leaf_size)
    far_square = far_blocks.reshape(leaves_dev, far_blocks.shape[1], rank_width, rank_width)
    order_row = perm[0]
    col_local = loc_col[0].astype(jnp.float32)
    row_local = loc_row[0].astype(jnp.float32)
    sub_bits = lax.axis_size("sub").bit_length() - 1
    leaf_bits = lax.axis_size("leaf").bit_length() - 1
    sub_pos = lax.axis_index("sub")
    leaf_pos = lax.axis_index("leaf")

    def combine_level(nodes):
        pairs = nodes.reshape(nodes.shape[0] // 2, 2, *nodes.shape[1:])
        return apply_up(up_col[0], pairs[:, 0]) + apply_up(up_col[1], pairs[:, 1])

    def group_levels(nodes, pos, bits, records, last):
        for bit_num in range(bits):
            here = pos >> bit_num
            sibling = lax.dynamic_index_in_dim(nodes, here ^ 1, 0, keepdims=False)
            records.append((sibling, here & 1))
            if not (last and bit_num + 1 == bits):
                nodes = combine_level(nodes)
        return nodes

    def climb_tree(root_coeff):
        records = []
        sub_nodes = lax.all_gather(root_coeff, "sub")
        group_root = group_levels(sub_nodes, sub_pos, sub_bits, records, False)[0]
        leaf_nodes = lax.all_gather(group_root, "leaf")
        group_levels(leaf_nodes, leaf_pos, leaf_bits, records, True)
        return records

    def descend_tree(records, columns):
        field_now = jnp.zeros((rank_width, columns), jnp.float32)
        for sibling, side_bit in reversed(records):
            row_pick = lax.dynamic_index_in_dim(up_row, side_bit, 0, keepdims=False)
            cpl_pick = lax.dynamic_index_in_dim(up_cpl, side_bit, 0, keepdims=False)
            field_now = apply_down(row_pick, field_now) + apply_down(cpl_pick, sibling)
        return field_now

    def apply_image(vectors):
        columns = vectors.shape[0]
        ordered = jnp.take(vectors, order_row, axis=1).astype(jnp.bfloat16)
        leaf_blocks = ordered.reshape(columns, leaves_dev, leaf_size)
        x_window = extended(leaf_blocks, "sub", 1)
        leaf_coeff = jnp.einsum(
            "clp,lpk->lkc", leaf_blocks, col_basis, preferred_element_type=jnp.float32
        )
        leaf_round = leaf_coeff.astype(jnp.bfloat16)
        coeff_window = extended(leaf_round, "sub", 0)
        current = leaf_coeff
        offsets = []
        start_at = 0
        while current.shape[0] > 1:
            node_count = current.shape[0]
            moved_up = apply_up(col_local[start_at : start_at + node_count], current)
            paired = moved_up.reshape(node_count // 2, 2, rank_width, columns)
            current = paired[:, 0] + paired[:, 1]
            offsets.append(start_at)
            start_at = start_at + node_count
        records = climb_tree(current[0])
        local_field = descend_tree(records, columns)[None]
        for start_at in reversed(offsets):
            node_count = local_field.shape[0] * 2
            local_field = apply_down(
                row_local[start_at : start_at + node_count], jnp.repeat(local_field, 2, axis=0)
            )
        width_all = 3 * leaves_dev
        far_live = far_index < width_all
        far_safe = jnp.minimum(far_index, width_all - 1)
        picked = coeff_window[far_safe]
        far_terms = jnp.einsum(
            "lkab,lkbc->lkac", far_square, picked, preferred_element_type=jnp.float32
        )
        far_weight = jnp.where(far_live, far_scale, jnp.zeros_like(far_scale))
        leaf_field = local_field + jnp.einsum(
            "lkac,lk->lac", far_terms, far_weight, precision=best_precision
        )
        field_round = leaf_field.astype(jnp.bfloat16)
        far_out = jnp.einsum(
            "lpk,lkc->clp", row_basis, field_round, preferred_element_type=jnp.float32
        )
        near_live = near_index < width_all
        near_safe = jnp.minimum(near_index, width_all - 1)
        near_pick = x_window[:, near_safe]
        near_terms = jnp.einsum(
            "lkpq,clkq->clkp", near_square, near_pick, preferred_element_type=jnp.float32
        )
        near_weight = jnp.where(near_live, near_scale, jnp.zeros_like(near_scale))
        near_sum = jnp.einsum("clkp,lk->clp", near_terms, near_weight, precision=best_precision)
        image = (far_out + near_sum).reshape(columns, leaves_dev * leaf_size)
        return jnp.zeros_like(image).at[:, order_row].set(image)

    rhs = p_dirs.shape[0]
    both = apply_image(jnp.concatenate([p_dirs, resid], axis=0))
    return (both[:rhs], both[rhs:])


def solution(mesh):
    return jax.shard_map(
        shards,
        mesh=mesh,
        in_specs=(
            P(None, ("leaf", "sub")),
            P(None, ("leaf", "sub")),
            P(("leaf", "sub"), None),
            P(("leaf", "sub"), None, None),
            P(("leaf", "sub"), None, None),
            P(("leaf", "sub"), None, None),
            P(("leaf", "sub"), None),
            P(("leaf", "sub"), None),
            P(("leaf", "sub"), None, None),
            P(("leaf", "sub"), None),
            P(("leaf", "sub"), None),
            P(("leaf", "sub"), None, None, None),
            P(("leaf", "sub"), None, None, None),
            P(),
            P(),
            P(),
        ),
        out_specs=(P(None, ("leaf", "sub")), P(None, ("leaf", "sub"))),
        check_vma=False,
    )
```

```python
import jax
import jax.numpy as jnp
from jax import lax
from jax.sharding import PartitionSpec as P

best_precision = lax.Precision.HIGHEST
LEAF_AXES = ("lx", "ly")
SUB_AXES = ("lz", "lc")
CLIMB_AXES = ("lc", "lz", "ly", "lx")


def extended(block, axis, dim):
    count = 1
    for name in axis:
        count = count * lax.axis_size(name)
    forward = [(i, i + 1) for i in range(count - 1)]
    backward = [(target, source) for source, target in forward]
    low = lax.ppermute(block, axis, forward)
    high = lax.ppermute(block, axis, backward)
    return jnp.concatenate([low, block, high], axis=dim)


def apply_up(matrix, coeffs):
    return jnp.einsum("...ab,...ac->...bc", matrix, coeffs, precision=best_precision)


def apply_down(matrix, coeffs):
    return jnp.einsum("...ab,...bc->...ac", matrix, coeffs, precision=best_precision)


def shards(
    p_dirs,
    resid,
    perm,
    col_basis,
    row_basis,
    near_blocks,
    near_scale,
    near_index,
    far_blocks,
    far_scale,
    far_index,
    loc_col,
    loc_row,
    up_col,
    up_row,
    up_cpl,
):
    leaves_dev, leaf_size, rank_width = col_basis.shape
    near_square = near_blocks.reshape(leaves_dev, near_blocks.shape[1], leaf_size, leaf_size)
    far_square = far_blocks.reshape(leaves_dev, far_blocks.shape[1], rank_width, rank_width)
    order_row = perm[0]
    col_local = loc_col[0].astype(jnp.float32)
    row_local = loc_row[0].astype(jnp.float32)

    def combine_level(nodes):
        pairs = nodes.reshape(nodes.shape[0] // 2, 2, *nodes.shape[1:])
        return apply_up(up_col[0], pairs[:, 0]) + apply_up(up_col[1], pairs[:, 1])

    def group_levels(nodes, pos, bits, records, last):
        for bit_num in range(bits):
            here = pos >> bit_num
            sibling = lax.dynamic_index_in_dim(nodes, here ^ 1, 0, keepdims=False)
            records.append((sibling, here & 1))
            if not (last and bit_num + 1 == bits):
                nodes = combine_level(nodes)
        return nodes

    def climb_tree(root_coeff):
        records = []
        node = root_coeff
        for step, name in enumerate(CLIMB_AXES):
            bits = lax.axis_size(name).bit_length() - 1
            gathered = lax.all_gather(node, name)
            last = step + 1 == len(CLIMB_AXES)
            node = group_levels(gathered, lax.axis_index(name), bits, records, last)[0]
        return records

    def descend_tree(records, columns):
        field_now = jnp.zeros((rank_width, columns), jnp.float32)
        for sibling, side_bit in reversed(records):
            row_pick = lax.dynamic_index_in_dim(up_row, side_bit, 0, keepdims=False)
            cpl_pick = lax.dynamic_index_in_dim(up_cpl, side_bit, 0, keepdims=False)
            field_now = apply_down(row_pick, field_now) + apply_down(cpl_pick, sibling)
        return field_now

    def apply_image(vectors):
        columns = vectors.shape[0]
        ordered = jnp.take(vectors, order_row, axis=1).astype(jnp.bfloat16)
        leaf_blocks = ordered.reshape(columns, leaves_dev, leaf_size)
        x_window = extended(leaf_blocks, SUB_AXES, 1)
        leaf_coeff = jnp.einsum(
            "clp,lpk->lkc", leaf_blocks, col_basis, preferred_element_type=jnp.float32
        )
        leaf_round = leaf_coeff.astype(jnp.bfloat16)
        coeff_window = extended(leaf_round, SUB_AXES, 0)
        current = leaf_coeff
        offsets = []
        start_at = 0
        while current.shape[0] > 1:
            node_count = current.shape[0]
            moved_up = apply_up(col_local[start_at : start_at + node_count], current)
            paired = moved_up.reshape(node_count // 2, 2, rank_width, columns)
            current = paired[:, 0] + paired[:, 1]
            offsets.append(start_at)
            start_at = start_at + node_count
        records = climb_tree(current[0])
        local_field = descend_tree(records, columns)[None]
        for start_at in reversed(offsets):
            node_count = local_field.shape[0] * 2
            local_field = apply_down(
                row_local[start_at : start_at + node_count], jnp.repeat(local_field, 2, axis=0)
            )
        width_all = 3 * leaves_dev
        far_live = far_index < width_all
        far_safe = jnp.minimum(far_index, width_all - 1)
        picked = coeff_window[far_safe]
        far_terms = jnp.einsum(
            "lkab,lkbc->lkac", far_square, picked, preferred_element_type=jnp.float32
        )
        far_weight = jnp.where(far_live, far_scale, jnp.zeros_like(far_scale))
        leaf_field = local_field + jnp.einsum(
            "lkac,lk->lac", far_terms, far_weight, precision=best_precision
        )
        field_round = leaf_field.astype(jnp.bfloat16)
        far_out = jnp.einsum(
            "lpk,lkc->clp", row_basis, field_round, preferred_element_type=jnp.float32
        )
        near_live = near_index < width_all
        near_safe = jnp.minimum(near_index, width_all - 1)
        near_pick = x_window[:, near_safe]
        near_terms = jnp.einsum(
            "lkpq,clkq->clkp", near_square, near_pick, preferred_element_type=jnp.float32
        )
        near_weight = jnp.where(near_live, near_scale, jnp.zeros_like(near_scale))
        near_sum = jnp.einsum("clkp,lk->clp", near_terms, near_weight, precision=best_precision)
        image = (far_out + near_sum).reshape(columns, leaves_dev * leaf_size)
        return jnp.zeros_like(image).at[:, order_row].set(image)

    rhs = p_dirs.shape[0]
    both = apply_image(jnp.concatenate([p_dirs, resid], axis=0))
    return (both[:rhs], both[rhs:])


def split_mesh(mesh):
    grid = mesh.devices
    n_leaf, n_sub = grid.shape
    n_x = len({dev.coords[0] for dev in grid[:, 0]})
    n_z = len({dev.coords[2] for dev in grid[0, :]})
    cube = grid.reshape(n_x, n_leaf // n_x, n_z, n_sub // n_z)
    return jax.sharding.Mesh(cube, LEAF_AXES + SUB_AXES)


def solution(mesh):
    flat = LEAF_AXES + SUB_AXES
    rows = P(flat, None)
    return jax.shard_map(
        shards,
        mesh=split_mesh(mesh),
        in_specs=(
            P(None, flat),
            P(None, flat),
            rows,
            P(flat, None, None),
            P(flat, None, None),
            P(flat, None, None),
            rows,
            rows,
            P(flat, None, None),
            rows,
            rows,
            P(flat, None, None, None),
            P(flat, None, None, None),
            P(),
            P(),
            P(),
        ),
        out_specs=(P(None, flat), P(None, flat)),
        check_vma=False,
    )
```

```python
import jax
import jax.numpy as jnp
from jax import lax
from jax.sharding import PartitionSpec as P

best_precision = lax.Precision.HIGHEST
LEAF_AXES = ("lx", "ly")
SUB_AXES = ("lz", "lc")
CLIMB_AXES = (SUB_AXES, LEAF_AXES)


def extended(block, axis, dim):
    count = 1
    for name in axis:
        count = count * lax.axis_size(name)
    forward = [(i, i + 1) for i in range(count - 1)]
    backward = [(target, source) for source, target in forward]
    low = lax.ppermute(block, axis, forward)
    high = lax.ppermute(block, axis, backward)
    return jnp.concatenate([low, block, high], axis=dim)


def apply_up(matrix, coeffs):
    return jnp.einsum("...ab,...ac->...bc", matrix, coeffs, precision=best_precision)


def apply_down(matrix, coeffs):
    return jnp.einsum("...ab,...bc->...ac", matrix, coeffs, precision=best_precision)


def shards(
    p_dirs,
    resid,
    perm,
    col_basis,
    row_basis,
    near_blocks,
    near_scale,
    near_index,
    far_blocks,
    far_scale,
    far_index,
    loc_col,
    loc_row,
    up_col,
    up_row,
    up_cpl,
):
    leaves_dev, leaf_size, rank_width = col_basis.shape
    near_square = near_blocks.reshape(leaves_dev, near_blocks.shape[1], leaf_size, leaf_size)
    far_square = far_blocks.reshape(leaves_dev, far_blocks.shape[1], rank_width, rank_width)
    order_row = perm[0]
    col_local = loc_col[0].astype(jnp.float32)
    row_local = loc_row[0].astype(jnp.float32)

    def combine_level(nodes):
        pairs = nodes.reshape(nodes.shape[0] // 2, 2, *nodes.shape[1:])
        return apply_up(up_col[0], pairs[:, 0]) + apply_up(up_col[1], pairs[:, 1])

    def group_levels(nodes, pos, bits, records, last):
        for bit_num in range(bits):
            here = pos >> bit_num
            sibling = lax.dynamic_index_in_dim(nodes, here ^ 1, 0, keepdims=False)
            records.append((sibling, here & 1))
            if not (last and bit_num + 1 == bits):
                nodes = combine_level(nodes)
        return nodes

    def climb_tree(root_coeff):
        records = []
        node = root_coeff
        for step, names in enumerate(CLIMB_AXES):
            count = 1
            pos = 0
            for name in names:
                count = count * lax.axis_size(name)
                pos = pos * lax.axis_size(name) + lax.axis_index(name)
            bits = count.bit_length() - 1
            slots = jnp.zeros((count,) + node.shape, node.dtype)
            gathered = lax.psum(lax.dynamic_update_index_in_dim(slots, node, pos, 0), names)
            last = step + 1 == len(CLIMB_AXES)
            node = group_levels(gathered, pos, bits, records, last)[0]
        return records

    def descend_tree(records, columns):
        field_now = jnp.zeros((rank_width, columns), jnp.float32)
        for sibling, side_bit in reversed(records):
            row_pick = lax.dynamic_index_in_dim(up_row, side_bit, 0, keepdims=False)
            cpl_pick = lax.dynamic_index_in_dim(up_cpl, side_bit, 0, keepdims=False)
            field_now = apply_down(row_pick, field_now) + apply_down(cpl_pick, sibling)
        return field_now

    def apply_image(vectors):
        columns = vectors.shape[0]
        ordered = jnp.take(vectors, order_row, axis=1).astype(jnp.bfloat16)
        leaf_blocks = ordered.reshape(columns, leaves_dev, leaf_size)
        x_window = extended(leaf_blocks, SUB_AXES, 1)
        leaf_coeff = jnp.einsum(
            "clp,lpk->lkc", leaf_blocks, col_basis, preferred_element_type=jnp.float32
        )
        leaf_round = leaf_coeff.astype(jnp.bfloat16)
        coeff_window = extended(leaf_round, SUB_AXES, 0)
        current = leaf_coeff
        offsets = []
        start_at = 0
        while current.shape[0] > 1:
            node_count = current.shape[0]
            moved_up = apply_up(col_local[start_at : start_at + node_count], current)
            paired = moved_up.reshape(node_count // 2, 2, rank_width, columns)
            current = paired[:, 0] + paired[:, 1]
            offsets.append(start_at)
            start_at = start_at + node_count
        records = climb_tree(current[0])
        local_field = descend_tree(records, columns)[None]
        for start_at in reversed(offsets):
            node_count = local_field.shape[0] * 2
            local_field = apply_down(
                row_local[start_at : start_at + node_count], jnp.repeat(local_field, 2, axis=0)
            )
        width_all = 3 * leaves_dev
        far_live = far_index < width_all
        far_safe = jnp.minimum(far_index, width_all - 1)
        picked = coeff_window[far_safe]
        far_terms = jnp.einsum(
            "lkab,lkbc->lkac", far_square, picked, preferred_element_type=jnp.float32
        )
        far_weight = jnp.where(far_live, far_scale, jnp.zeros_like(far_scale))
        leaf_field = local_field + jnp.einsum(
            "lkac,lk->lac", far_terms, far_weight, precision=best_precision
        )
        field_round = leaf_field.astype(jnp.bfloat16)
        far_out = jnp.einsum(
            "lpk,lkc->clp", row_basis, field_round, preferred_element_type=jnp.float32
        )
        near_live = near_index < width_all
        near_safe = jnp.minimum(near_index, width_all - 1)
        near_pick = x_window[:, near_safe]
        near_terms = jnp.einsum(
            "lkpq,clkq->clkp", near_square, near_pick, preferred_element_type=jnp.float32
        )
        near_weight = jnp.where(near_live, near_scale, jnp.zeros_like(near_scale))
        near_sum = jnp.einsum("clkp,lk->clp", near_terms, near_weight, precision=best_precision)
        image = (far_out + near_sum).reshape(columns, leaves_dev * leaf_size)
        return jnp.zeros_like(image).at[:, order_row].set(image)

    rhs = p_dirs.shape[0]
    both = apply_image(jnp.concatenate([p_dirs, resid], axis=0))
    return (both[:rhs], both[rhs:])


def split_mesh(mesh):
    grid = mesh.devices
    n_leaf, n_sub = grid.shape
    n_x = len({dev.coords[0] for dev in grid[:, 0]})
    n_z = len({dev.coords[2] for dev in grid[0, :]})
    cube = grid.reshape(n_x, n_leaf // n_x, n_z, n_sub // n_z)
    return jax.sharding.Mesh(cube, LEAF_AXES + SUB_AXES)


def solution(mesh):
    flat = LEAF_AXES + SUB_AXES
    rows = P(flat, None)
    return jax.shard_map(
        shards,
        mesh=split_mesh(mesh),
        in_specs=(
            P(None, flat),
            P(None, flat),
            rows,
            P(flat, None, None),
            P(flat, None, None),
            P(flat, None, None),
            rows,
            rows,
            P(flat, None, None),
            rows,
            rows,
            P(flat, None, None, None),
            P(flat, None, None, None),
            P(),
            P(),
            P(),
        ),
        out_specs=(P(None, flat), P(None, flat)),
        check_vma=False,
    )
```

```python
import jax
import jax.numpy as jnp
from jax import lax
from jax.sharding import PartitionSpec as P

best_precision = lax.Precision.HIGHEST
LEAF_AXES = ("lx", "ly")
SUB_AXES = ("lz", "lc")
CLIMB_AXES = ("lc", "lz", "ly", "lx")


def from_partner(value, axis, distance):
    mask = 2**distance
    pairs = [(source, source ^ mask) for source in range(lax.axis_size(axis))]
    return lax.ppermute(value, axis, pairs)


def extended(block, axis, dim):
    count = 1
    for name in axis:
        count = count * lax.axis_size(name)
    forward = [(i, i + 1) for i in range(count - 1)]
    backward = [(target, source) for source, target in forward]
    low = lax.ppermute(block, axis, forward)
    high = lax.ppermute(block, axis, backward)
    return jnp.concatenate([low, block, high], axis=dim)


def apply_up(matrix, coeffs):
    return jnp.einsum("...ab,...ac->...bc", matrix, coeffs, precision=best_precision)


def apply_down(matrix, coeffs):
    return jnp.einsum("...ab,...bc->...ac", matrix, coeffs, precision=best_precision)


def shards(
    p_dirs,
    resid,
    perm,
    col_basis,
    row_basis,
    near_blocks,
    near_scale,
    near_index,
    far_blocks,
    far_scale,
    far_index,
    loc_col,
    loc_row,
    up_col,
    up_row,
    up_cpl,
):
    leaves_dev, leaf_size, rank_width = col_basis.shape
    near_square = near_blocks.reshape(leaves_dev, near_blocks.shape[1], leaf_size, leaf_size)
    far_square = far_blocks.reshape(leaves_dev, far_blocks.shape[1], rank_width, rank_width)
    order_row = perm[0]
    col_local = loc_col[0].astype(jnp.float32)
    row_local = loc_row[0].astype(jnp.float32)

    def side_pick(table, side_bit):
        return lax.dynamic_index_in_dim(table, side_bit, 0, keepdims=False)

    def climb_tree(root_coeff, tied):
        current = root_coeff
        field_sum = None
        path_rows = None
        level = 0
        for step, name in enumerate(CLIMB_AXES):
            bits = lax.axis_size(name).bit_length() - 1
            for bit_num in range(bits):
                sibling = from_partner(current, name, bit_num)
                side_bit = lax.axis_index(name) >> bit_num & 1
                term = apply_down(side_pick(up_cpl, side_bit), sibling)
                if path_rows is None:
                    field_sum = term
                    path_rows = side_pick(up_row, side_bit)
                else:
                    field_sum = field_sum + apply_down(path_rows, term)
                    path_rows = apply_down(path_rows, side_pick(up_row, side_bit))
                if step + 1 < len(CLIMB_AXES) or bit_num + 1 < bits:
                    left_part = jnp.where(side_bit == 1, sibling, current)
                    right_part = jnp.where(side_bit == 1, current, sibling)
                    current = apply_up(up_col[0], left_part) + apply_up(up_col[1], right_part)
                    if level < len(tied):
                        current, tied[level] = lax.optimization_barrier((current, tied[level]()))
                level += 1
        return field_sum

    def apply_image(vectors):
        columns = vectors.shape[0]
        ordered = jnp.take(vectors, order_row, axis=1).astype(jnp.bfloat16)
        leaf_blocks = ordered.reshape(columns, leaves_dev, leaf_size)
        x_window = extended(leaf_blocks, SUB_AXES, 1)
        leaf_coeff = jnp.einsum(
            "clp,lpk->lkc", leaf_blocks, col_basis, preferred_element_type=jnp.float32
        )
        leaf_round = leaf_coeff.astype(jnp.bfloat16)
        coeff_window = extended(leaf_round, SUB_AXES, 0)
        current = leaf_coeff
        offsets = []
        start_at = 0
        while current.shape[0] > 1:
            node_count = current.shape[0]
            moved_up = apply_up(col_local[start_at : start_at + node_count], current)
            paired = moved_up.reshape(node_count // 2, 2, rank_width, columns)
            current = paired[:, 0] + paired[:, 1]
            offsets.append(start_at)
            start_at = start_at + node_count
        width_all = 3 * leaves_dev

        def leaf_paths():
            paths = None
            for start_at in reversed(offsets):
                node_count = 2 if paths is None else paths.shape[0] * 2
                rows = row_local[start_at : start_at + node_count]
                if paths is None:
                    paths = rows
                else:
                    paths = apply_down(rows, jnp.repeat(paths, 2, axis=0))
            return paths

        def far_part(lo, hi):
            def run():
                idx = far_index[lo:hi]
                far_live = idx < width_all
                picked = coeff_window[jnp.minimum(idx, width_all - 1)]
                far_terms = jnp.einsum(
                    "lkab,lkbc->lkac", far_square[lo:hi], picked, preferred_element_type=jnp.float32
                )
                far_weight = jnp.where(far_live, far_scale[lo:hi], jnp.zeros_like(far_scale[lo:hi]))
                return jnp.einsum("lkac,lk->lac", far_terms, far_weight, precision=best_precision)
            return run

        def near_part(lo, hi):
            def run():
                idx = near_index[lo:hi]
                near_live = idx < width_all
                near_pick = x_window[:, jnp.minimum(idx, width_all - 1)]
                near_terms = jnp.einsum(
                    "lkpq,clkq->clkp", near_square[lo:hi], near_pick, preferred_element_type=jnp.float32
                )
                near_weight = jnp.where(near_live, near_scale[lo:hi], jnp.zeros_like(near_scale[lo:hi]))
                return jnp.einsum("clkp,lk->clp", near_terms, near_weight, precision=best_precision)
            return run

        half = leaves_dev // 2
        quarter = leaves_dev // 4
        tied = [leaf_paths, far_part(0, half), far_part(half, leaves_dev)]
        tied += [near_part(i * quarter, (i + 1) * quarter) for i in range(4)]
        root_field = climb_tree(current[0], tied)
        tied = [part() if callable(part) else part for part in tied]
        paths = tied[0]
        far_acc = jnp.concatenate(tied[1:3], axis=0)
        near_sum = jnp.concatenate(tied[3:7], axis=1)
        local_field = apply_down(paths, jnp.broadcast_to(root_field, (leaves_dev,) + root_field.shape))
        leaf_field = local_field + far_acc
        field_round = leaf_field.astype(jnp.bfloat16)
        far_out = jnp.einsum(
            "lpk,lkc->clp", row_basis, field_round, preferred_element_type=jnp.float32
        )
        image = (far_out + near_sum).reshape(columns, leaves_dev * leaf_size)
        return jnp.zeros_like(image).at[:, order_row].set(image)

    rhs = p_dirs.shape[0]
    both = apply_image(jnp.concatenate([p_dirs, resid], axis=0))
    return (both[:rhs], both[rhs:])


def split_mesh(mesh):
    grid = mesh.devices
    n_leaf, n_sub = grid.shape
    n_x = len({dev.coords[0] for dev in grid[:, 0]})
    n_z = len({dev.coords[2] for dev in grid[0, :]})
    cube = grid.reshape(n_x, n_leaf // n_x, n_z, n_sub // n_z)
    return jax.sharding.Mesh(cube, LEAF_AXES + SUB_AXES)


def solution(mesh):
    flat = LEAF_AXES + SUB_AXES
    rows = P(flat, None)
    return jax.shard_map(
        shards,
        mesh=split_mesh(mesh),
        in_specs=(
            P(None, flat),
            P(None, flat),
            rows,
            P(flat, None, None),
            P(flat, None, None),
            P(flat, None, None),
            rows,
            rows,
            P(flat, None, None),
            rows,
            rows,
            P(flat, None, None, None),
            P(flat, None, None, None),
            P(),
            P(),
            P(),
        ),
        out_specs=(P(None, flat), P(None, flat)),
        check_vma=False,
    )
```

```python
import jax
import jax.numpy as jnp
from jax import lax
from jax.sharding import PartitionSpec as P

best_precision = lax.Precision.HIGHEST
LEAF_AXES = ("lx", "ly")
SUB_AXES = ("lz", "lc")
CLIMB_AXES = ("lc", "lz", "ly", "lx")


def from_partner(value, axis, distance):
    mask = 2**distance
    pairs = [(source, source ^ mask) for source in range(lax.axis_size(axis))]
    return lax.ppermute(value, axis, pairs)


def extended(block, axis, dim):
    count = 1
    for name in axis:
        count = count * lax.axis_size(name)
    forward = [(i, i + 1) for i in range(count - 1)]
    backward = [(target, source) for source, target in forward]
    low = lax.ppermute(block, axis, forward)
    high = lax.ppermute(block, axis, backward)
    return jnp.concatenate([low, block, high], axis=dim)


def apply_up(matrix, coeffs):
    return jnp.einsum("...ab,...ac->...bc", matrix, coeffs, precision=best_precision)


def apply_down(matrix, coeffs):
    return jnp.einsum("...ab,...bc->...ac", matrix, coeffs, precision=best_precision)


def shards(
    p_dirs,
    resid,
    perm,
    col_basis,
    row_basis,
    near_blocks,
    near_scale,
    near_index,
    far_blocks,
    far_scale,
    far_index,
    loc_col,
    loc_row,
    up_col,
    up_row,
    up_cpl,
):
    leaves_dev, leaf_size, rank_width = col_basis.shape
    near_square = near_blocks.reshape(leaves_dev, near_blocks.shape[1], leaf_size, leaf_size)
    far_square = far_blocks.reshape(leaves_dev, far_blocks.shape[1], rank_width, rank_width)
    order_row = perm[0]
    col_local = loc_col[0].astype(jnp.float32)
    row_local = loc_row[0].astype(jnp.float32)

    def climb_sides():
        sides = []
        for name in CLIMB_AXES:
            for bit_num in range(lax.axis_size(name).bit_length() - 1):
                sides.append((name, bit_num, lax.axis_index(name) >> bit_num & 1))
        return sides

    def pick(table, side_col):
        return jnp.where(side_col[:, None, None] == 1, table[1][None], table[0][None])

    def field_weights(side_col):
        level_count = side_col.shape[0]
        row_sel = pick(up_row, side_col)
        eye = jnp.broadcast_to(jnp.eye(rank_width, dtype=jnp.float32), row_sel.shape)
        prefix = row_sel
        shift = 1
        while shift < level_count:
            earlier = jnp.concatenate([eye[:shift], prefix[:-shift]], axis=0)
            prefix = apply_down(earlier, prefix)
            shift *= 2
        before = jnp.concatenate([eye[:1], prefix[:-1]], axis=0)
        weights = apply_down(before, pick(up_cpl, side_col))
        return weights.transpose(1, 0, 2).reshape(rank_width, level_count * rank_width)

    def climb_tree(root_coeff):
        sides = climb_sides()
        side_col = jnp.stack([side for _, _, side in sides])
        own_first = jnp.concatenate([pick(up_col, side_col), pick(up_col, 1 - side_col)], axis=1)
        current = root_coeff
        siblings = []
        for level, (name, bit_num, _) in enumerate(sides):
            sibling = from_partner(current, name, bit_num)
            siblings.append(sibling)
            if level + 1 < len(sides):
                stacked = jnp.concatenate([current, sibling], axis=0)
                current = apply_up(own_first[level], stacked)
        stacked = jnp.concatenate(siblings, axis=0)
        return apply_down(field_weights(side_col), stacked)

    def apply_image(vectors):
        columns = vectors.shape[0]
        ordered = jnp.take(vectors, order_row, axis=1).astype(jnp.bfloat16)
        leaf_blocks = ordered.reshape(columns, leaves_dev, leaf_size)
        x_window = extended(leaf_blocks, SUB_AXES, 1)
        leaf_coeff = jnp.einsum(
            "clp,lpk->lkc", leaf_blocks, col_basis, preferred_element_type=jnp.float32
        )
        leaf_round = leaf_coeff.astype(jnp.bfloat16)
        coeff_window = extended(leaf_round, SUB_AXES, 0)
        current = leaf_coeff
        offsets = []
        start_at = 0
        while current.shape[0] > 1:
            node_count = current.shape[0]
            moved_up = apply_up(col_local[start_at : start_at + node_count], current)
            paired = moved_up.reshape(node_count // 2, 2, rank_width, columns)
            current = paired[:, 0] + paired[:, 1]
            offsets.append(start_at)
            start_at = start_at + node_count
        width_all = 3 * leaves_dev
        paths = None
        for start_at in reversed(offsets):
            node_count = 2 if paths is None else paths.shape[0] * 2
            rows = row_local[start_at : start_at + node_count]
            paths = rows if paths is None else apply_down(rows, jnp.repeat(paths, 2, axis=0))
        root_field = climb_tree(current[0])
        local_field = apply_down(paths, jnp.broadcast_to(root_field, (leaves_dev,) + root_field.shape))
        far_live = far_index < width_all
        picked = coeff_window[jnp.minimum(far_index, width_all - 1)]
        far_terms = jnp.einsum(
            "lkab,lkbc->lkac", far_square, picked, preferred_element_type=jnp.float32
        )
        far_weight = jnp.where(far_live, far_scale, jnp.zeros_like(far_scale))
        leaf_field = local_field + jnp.einsum(
            "lkac,lk->lac", far_terms, far_weight, precision=best_precision
        )
        field_round = leaf_field.astype(jnp.bfloat16)
        far_out = jnp.einsum(
            "lpk,lkc->clp", row_basis, field_round, preferred_element_type=jnp.float32
        )
        near_live = near_index < width_all
        near_pick = x_window[:, jnp.minimum(near_index, width_all - 1)]
        near_terms = jnp.einsum(
            "lkpq,clkq->clkp", near_square, near_pick, preferred_element_type=jnp.float32
        )
        near_weight = jnp.where(near_live, near_scale, jnp.zeros_like(near_scale))
        near_sum = jnp.einsum("clkp,lk->clp", near_terms, near_weight, precision=best_precision)
        image = (far_out + near_sum).reshape(columns, leaves_dev * leaf_size)
        return jnp.zeros_like(image).at[:, order_row].set(image)

    rhs = p_dirs.shape[0]
    both = apply_image(jnp.concatenate([p_dirs, resid], axis=0))
    return (both[:rhs], both[rhs:])


def split_mesh(mesh):
    grid = mesh.devices
    n_leaf, n_sub = grid.shape
    n_x = len({dev.coords[0] for dev in grid[:, 0]})
    n_z = len({dev.coords[2] for dev in grid[0, :]})
    cube = grid.reshape(n_x, n_leaf // n_x, n_z, n_sub // n_z)
    return jax.sharding.Mesh(cube, LEAF_AXES + SUB_AXES)


def solution(mesh):
    flat = LEAF_AXES + SUB_AXES
    rows = P(flat, None)
    return jax.shard_map(
        shards,
        mesh=split_mesh(mesh),
        in_specs=(
            P(None, flat),
            P(None, flat),
            rows,
            P(flat, None, None),
            P(flat, None, None),
            P(flat, None, None),
            rows,
            rows,
            P(flat, None, None),
            rows,
            rows,
            P(flat, None, None, None),
            P(flat, None, None, None),
            P(),
            P(),
            P(),
        ),
        out_specs=(P(None, flat), P(None, flat)),
        check_vma=False,
    )
```

```python
import jax
import jax.numpy as jnp
from jax import lax
from jax.sharding import PartitionSpec as P

best_precision = lax.Precision.HIGHEST
LEAF_AXES = ("lx", "ly")
SUB_AXES = ("lz", "lc")
CLIMB_AXES = ("lc", "lz", "ly", "lx")


def from_partner(value, axis, distance):
    mask = 2**distance
    pairs = [(source, source ^ mask) for source in range(lax.axis_size(axis))]
    return lax.ppermute(value, axis, pairs)


def extended(block, axis, dim):
    count = 1
    for name in axis:
        count = count * lax.axis_size(name)
    forward = [(i, i + 1) for i in range(count - 1)]
    backward = [(target, source) for source, target in forward]
    low = lax.ppermute(block, axis, forward)
    high = lax.ppermute(block, axis, backward)
    return jnp.concatenate([low, block, high], axis=dim)


def apply_up(matrix, coeffs):
    return jnp.einsum("...ab,...ac->...bc", matrix, coeffs, precision=best_precision)


def apply_down(matrix, coeffs):
    return jnp.einsum("...ab,...bc->...ac", matrix, coeffs, precision=best_precision)


def shards(
    p_dirs,
    resid,
    perm,
    col_basis,
    row_basis,
    near_blocks,
    near_scale,
    near_index,
    far_blocks,
    far_scale,
    far_index,
    loc_col,
    loc_row,
    up_col,
    up_row,
    up_cpl,
):
    leaves_dev, leaf_size, rank_width = col_basis.shape
    order_row = perm[0]
    col_local = loc_col[0].astype(jnp.float32)
    row_local = loc_row[0].astype(jnp.float32)

    def climb_sides():
        sides = []
        for name in CLIMB_AXES:
            for bit_num in range(lax.axis_size(name).bit_length() - 1):
                sides.append((name, bit_num, lax.axis_index(name) >> bit_num & 1))
        return sides

    def pick(table, side_col):
        return jnp.where(side_col[:, None, None] == 1, table[1][None], table[0][None])

    def field_weights(side_col):
        level_count = side_col.shape[0]
        row_sel = pick(up_row, side_col)
        eye = jnp.broadcast_to(jnp.eye(rank_width, dtype=jnp.float32), row_sel.shape)
        prefix = row_sel
        shift = 1
        while shift < level_count:
            earlier = jnp.concatenate([eye[:shift], prefix[:-shift]], axis=0)
            prefix = apply_down(earlier, prefix)
            shift *= 2
        before = jnp.concatenate([eye[:1], prefix[:-1]], axis=0)
        weights = apply_down(before, pick(up_cpl, side_col))
        return weights.transpose(1, 0, 2).reshape(rank_width, level_count * rank_width)

    def climb_tree(root_coeff, stages, results):
        sides = climb_sides()
        side_col = jnp.stack([side for _, _, side in sides])
        own_first = jnp.concatenate([pick(up_col, side_col), pick(up_col, 1 - side_col)], axis=1)
        current = root_coeff
        siblings = []
        for level, (name, bit_num, _) in enumerate(sides):
            sibling = from_partner(current, name, bit_num)
            if level < len(stages):
                key, stage = stages[level]
                sibling, results[key] = lax.optimization_barrier((sibling, stage()))
            siblings.append(sibling)
            if level + 1 < len(sides):
                stacked = jnp.concatenate([current, sibling], axis=0)
                current = apply_up(own_first[level], stacked)
        stacked = jnp.concatenate(siblings, axis=0)
        return apply_down(field_weights(side_col), stacked)

    def apply_image(vectors):
        columns = vectors.shape[0]
        ordered = jnp.take(vectors, order_row, axis=1).astype(jnp.bfloat16)
        leaf_blocks = ordered.reshape(columns, leaves_dev, leaf_size)
        x_window = extended(leaf_blocks, SUB_AXES, 1)
        leaf_coeff = jnp.einsum(
            "clp,lpk->lkc", leaf_blocks, col_basis, preferred_element_type=jnp.float32
        )
        leaf_round = leaf_coeff.astype(jnp.bfloat16)
        coeff_window = extended(leaf_round, SUB_AXES, 0)
        current = leaf_coeff
        offsets = []
        start_at = 0
        while current.shape[0] > 1:
            node_count = current.shape[0]
            moved_up = apply_up(col_local[start_at : start_at + node_count], current)
            paired = moved_up.reshape(node_count // 2, 2, rank_width, columns)
            current = paired[:, 0] + paired[:, 1]
            offsets.append(start_at)
            start_at = start_at + node_count
        width_all = 3 * leaves_dev
        results = {}

        def leaf_paths():
            paths = None
            for start_at in reversed(offsets):
                node_count = 2 if paths is None else paths.shape[0] * 2
                rows = row_local[start_at : start_at + node_count]
                paths = rows if paths is None else apply_down(rows, jnp.repeat(paths, 2, axis=0))
            return paths

        def near_square():
            return near_blocks.reshape(leaves_dev, near_blocks.shape[1], leaf_size, leaf_size)

        def far_square():
            return far_blocks.reshape(leaves_dev, far_blocks.shape[1], rank_width, rank_width)

        def far_picked():
            return coeff_window[jnp.minimum(far_index, width_all - 1)]

        def far_terms():
            return jnp.einsum(
                "lkab,lkbc->lkac", results["far_sq"], results["far_pick"],
                preferred_element_type=jnp.float32,
            )

        def far_sum():
            far_weight = jnp.where(far_index < width_all, far_scale, jnp.zeros_like(far_scale))
            return jnp.einsum("lkac,lk->lac", results["far_terms"], far_weight, precision=best_precision)

        def near_picked():
            return x_window[:, jnp.minimum(near_index, width_all - 1)]

        def near_terms():
            return jnp.einsum(
                "lkpq,clkq->clkp", results["near_sq"], results["near_pick"],
                preferred_element_type=jnp.float32,
            )

        def near_total():
            near_weight = jnp.where(near_index < width_all, near_scale, jnp.zeros_like(near_scale))
            return jnp.einsum("clkp,lk->clp", results["near_terms"], near_weight, precision=best_precision)

        stages = [
            ("near_sq", near_square),
            ("far_sq", far_square),
            ("far_pick", far_picked),
            ("far_terms", far_terms),
            ("far_sum", far_sum),
            ("near_pick", near_picked),
            ("near_terms", near_terms),
            ("near_sum", near_total),
            ("paths", leaf_paths),
        ]
        root_field = climb_tree(current[0], stages, results)
        for key, stage in stages:
            if key not in results:
                results[key] = stage()
        paths = results["paths"]
        near_sum = results["near_sum"]
        local_field = apply_down(paths, jnp.broadcast_to(root_field, (leaves_dev,) + root_field.shape))
        leaf_field = local_field + results["far_sum"]
        field_round = leaf_field.astype(jnp.bfloat16)
        far_out = jnp.einsum(
            "lpk,lkc->clp", row_basis, field_round, preferred_element_type=jnp.float32
        )
        image = (far_out + near_sum).reshape(columns, leaves_dev * leaf_size)
        return jnp.zeros_like(image).at[:, order_row].set(image)

    rhs = p_dirs.shape[0]
    both = apply_image(jnp.concatenate([p_dirs, resid], axis=0))
    return (both[:rhs], both[rhs:])


def split_mesh(mesh):
    grid = mesh.devices
    n_leaf, n_sub = grid.shape
    n_x = len({dev.coords[0] for dev in grid[:, 0]})
    n_z = len({dev.coords[2] for dev in grid[0, :]})
    cube = grid.reshape(n_x, n_leaf // n_x, n_z, n_sub // n_z)
    return jax.sharding.Mesh(cube, LEAF_AXES + SUB_AXES)


def solution(mesh):
    flat = LEAF_AXES + SUB_AXES
    rows = P(flat, None)
    return jax.shard_map(
        shards,
        mesh=split_mesh(mesh),
        in_specs=(
            P(None, flat),
            P(None, flat),
            rows,
            P(flat, None, None),
            P(flat, None, None),
            P(flat, None, None),
            rows,
            rows,
            P(flat, None, None),
            rows,
            rows,
            P(flat, None, None, None),
            P(flat, None, None, None),
            P(),
            P(),
            P(),
        ),
        out_specs=(P(None, flat), P(None, flat)),
        check_vma=False,
    )
```

```python
import jax
import jax.numpy as jnp
from jax import lax
from jax.sharding import PartitionSpec as P

best_precision = lax.Precision.HIGHEST
LEAF_AXES = ("lx", "ly")
SUB_AXES = ("lz", "lc")
CLIMB_AXES = ("lc", "lz", "ly", "lx")


def from_partner(value, axis, distance):
    mask = 2**distance
    pairs = [(source, source ^ mask) for source in range(lax.axis_size(axis))]
    return lax.ppermute(value, axis, pairs)


def extended(block, axis, dim):
    count = 1
    for name in axis:
        count = count * lax.axis_size(name)
    forward = [(i, i + 1) for i in range(count - 1)]
    backward = [(target, source) for source, target in forward]
    low = lax.ppermute(block, axis, forward)
    high = lax.ppermute(block, axis, backward)
    return jnp.concatenate([low, block, high], axis=dim)


def apply_up(matrix, coeffs):
    return jnp.einsum("...ab,...ac->...bc", matrix, coeffs, precision=best_precision)


def apply_down(matrix, coeffs):
    return jnp.einsum("...ab,...bc->...ac", matrix, coeffs, precision=best_precision)


def shards(
    p_dirs,
    resid,
    perm,
    col_basis,
    row_basis,
    near_blocks,
    near_scale,
    near_index,
    far_blocks,
    far_scale,
    far_index,
    loc_col,
    loc_row,
    up_col,
    up_row,
    up_cpl,
):
    leaves_dev, leaf_size, rank_width = col_basis.shape
    order_row = perm[0]
    col_local = loc_col[0].astype(jnp.float32)
    row_local = loc_row[0].astype(jnp.float32)

    def climb_sides():
        sides = []
        for name in CLIMB_AXES:
            for bit_num in range(lax.axis_size(name).bit_length() - 1):
                sides.append((name, bit_num, lax.axis_index(name) >> bit_num & 1))
        return sides

    def pick(table, side_col):
        return jnp.where(side_col[:, None, None] == 1, table[1][None], table[0][None])

    def field_weights(side_col):
        level_count = side_col.shape[0]
        row_sel = pick(up_row, side_col)
        eye = jnp.broadcast_to(jnp.eye(rank_width, dtype=jnp.float32), row_sel.shape)
        prefix = row_sel
        shift = 1
        while shift < level_count:
            earlier = jnp.concatenate([eye[:shift], prefix[:-shift]], axis=0)
            prefix = apply_down(earlier, prefix)
            shift *= 2
        before = jnp.concatenate([eye[:1], prefix[:-1]], axis=0)
        weights = apply_down(before, pick(up_cpl, side_col))
        return weights.transpose(1, 0, 2).reshape(rank_width, level_count * rank_width)

    def climb_tree(root_coeff, stages, results):
        sides = climb_sides()
        side_col = jnp.stack([side for _, _, side in sides])
        own_first = jnp.concatenate([pick(up_col, side_col), pick(up_col, 1 - side_col)], axis=1)
        current = root_coeff
        siblings = []
        for level, (name, bit_num, _) in enumerate(sides):
            sibling = from_partner(current, name, bit_num)
            if level < len(stages):
                key, stage = stages[level]
                sibling, results[key] = lax.optimization_barrier((sibling, stage()))
            siblings.append(sibling)
            if level + 1 < len(sides):
                stacked = jnp.concatenate([current, sibling], axis=0)
                current = apply_up(own_first[level], stacked)
        stacked = jnp.concatenate(siblings, axis=0)
        return apply_down(field_weights(side_col), stacked)

    def apply_image(vectors):
        columns = vectors.shape[0]
        ordered = jnp.take(vectors, order_row, axis=1).astype(jnp.bfloat16)
        leaf_blocks = ordered.reshape(columns, leaves_dev, leaf_size)
        x_window = extended(leaf_blocks, SUB_AXES, 1)
        leaf_coeff = jnp.einsum(
            "clp,lpk->lkc", leaf_blocks, col_basis, preferred_element_type=jnp.float32
        )
        leaf_round = leaf_coeff.astype(jnp.bfloat16)
        coeff_window = extended(leaf_round, SUB_AXES, 0)
        current = leaf_coeff
        offsets = []
        start_at = 0
        while current.shape[0] > 1:
            node_count = current.shape[0]
            moved_up = apply_up(col_local[start_at : start_at + node_count], current)
            paired = moved_up.reshape(node_count // 2, 2, rank_width, columns)
            current = paired[:, 0] + paired[:, 1]
            offsets.append(start_at)
            start_at = start_at + node_count
        width_all = 3 * leaves_dev
        results = {}

        def leaf_paths():
            paths = None
            for start_at in reversed(offsets):
                node_count = 2 if paths is None else paths.shape[0] * 2
                rows = row_local[start_at : start_at + node_count]
                paths = rows if paths is None else apply_down(rows, jnp.repeat(paths, 2, axis=0))
            return paths

        def near_square():
            return near_blocks.reshape(leaves_dev, near_blocks.shape[1], leaf_size, leaf_size)

        def far_square():
            return far_blocks.reshape(leaves_dev, far_blocks.shape[1], rank_width, rank_width)

        def far_picked():
            return coeff_window[jnp.minimum(far_index, width_all - 1)]

        def far_sum():
            far_weight = jnp.where(far_index < width_all, far_scale, jnp.zeros_like(far_scale))
            scaled = results["far_pick"].astype(jnp.float32) * far_weight[:, :, None, None]
            return jnp.einsum("lkab,lkbc->lac", results["far_sq"], scaled, precision=best_precision)

        def near_picked():
            return x_window[:, jnp.minimum(near_index, width_all - 1)]

        def near_total():
            near_weight = jnp.where(near_index < width_all, near_scale, jnp.zeros_like(near_scale))
            scaled = results["near_pick"].astype(jnp.float32) * near_weight[None, :, :, None]
            return jnp.einsum("lkpq,clkq->clp", results["near_sq"], scaled, precision=best_precision)

        stages = [
            ("near_sq", near_square),
            ("far_sq", far_square),
            ("far_pick", far_picked),
            ("far_sum", far_sum),
            ("near_pick", near_picked),
            ("near_sum", near_total),
            ("paths", leaf_paths),
        ]
        root_field = climb_tree(current[0], stages, results)
        for key, stage in stages:
            if key not in results:
                results[key] = stage()
        paths = results["paths"]
        near_sum = results["near_sum"]
        local_field = apply_down(paths, jnp.broadcast_to(root_field, (leaves_dev,) + root_field.shape))
        leaf_field = local_field + results["far_sum"]
        field_round = leaf_field.astype(jnp.bfloat16)
        far_out = jnp.einsum(
            "lpk,lkc->clp", row_basis, field_round, preferred_element_type=jnp.float32
        )
        image = (far_out + near_sum).reshape(columns, leaves_dev * leaf_size)
        return jnp.zeros_like(image).at[:, order_row].set(image)

    rhs = p_dirs.shape[0]
    both = apply_image(jnp.concatenate([p_dirs, resid], axis=0))
    return (both[:rhs], both[rhs:])


def split_mesh(mesh):
    grid = mesh.devices
    n_leaf, n_sub = grid.shape
    n_x = len({dev.coords[0] for dev in grid[:, 0]})
    n_z = len({dev.coords[2] for dev in grid[0, :]})
    cube = grid.reshape(n_x, n_leaf // n_x, n_z, n_sub // n_z)
    return jax.sharding.Mesh(cube, LEAF_AXES + SUB_AXES)


def solution(mesh):
    flat = LEAF_AXES + SUB_AXES
    rows = P(flat, None)
    return jax.shard_map(
        shards,
        mesh=split_mesh(mesh),
        in_specs=(
            P(None, flat),
            P(None, flat),
            rows,
            P(flat, None, None),
            P(flat, None, None),
            P(flat, None, None),
            rows,
            rows,
            P(flat, None, None),
            rows,
            rows,
            P(flat, None, None, None),
            P(flat, None, None, None),
            P(),
            P(),
            P(),
        ),
        out_specs=(P(None, flat), P(None, flat)),
        check_vma=False,
    )
```

```python
import jax
import jax.numpy as jnp
from jax import lax
from jax.sharding import PartitionSpec as P

best_precision = lax.Precision.HIGHEST
LEAF_AXES = ("lx", "ly")
SUB_AXES = ("lz", "lc")
CLIMB_AXES = ("lc", "lz", "ly", "lx")


def from_partner(value, axis, distance):
    mask = 2**distance
    pairs = [(source, source ^ mask) for source in range(lax.axis_size(axis))]
    return lax.ppermute(value, axis, pairs)


def extended(block, axis, dim):
    count = 1
    for name in axis:
        count = count * lax.axis_size(name)
    forward = [(i, i + 1) for i in range(count - 1)]
    backward = [(target, source) for source, target in forward]
    low = lax.ppermute(block, axis, forward)
    high = lax.ppermute(block, axis, backward)
    return jnp.concatenate([low, block, high], axis=dim)


def apply_up(matrix, coeffs):
    return jnp.einsum("...ab,...ac->...bc", matrix, coeffs, precision=best_precision)


def apply_down(matrix, coeffs):
    return jnp.einsum("...ab,...bc->...ac", matrix, coeffs, precision=best_precision)


def shards(
    p_dirs,
    resid,
    perm,
    col_basis,
    row_basis,
    near_blocks,
    near_scale,
    near_index,
    far_blocks,
    far_scale,
    far_index,
    loc_col,
    loc_row,
    up_col,
    up_row,
    up_cpl,
):
    leaves_dev, leaf_size, rank_width = col_basis.shape
    order_row = perm[0]
    col_local = loc_col[0].astype(jnp.float32)
    row_local = loc_row[0].astype(jnp.float32)

    def climb_sides():
        sides = []
        for name in CLIMB_AXES:
            for bit_num in range(lax.axis_size(name).bit_length() - 1):
                sides.append((name, bit_num, lax.axis_index(name) >> bit_num & 1))
        return sides

    def pick(table, side_col):
        return jnp.where(side_col[:, None, None] == 1, table[1][None], table[0][None])

    def field_weights(side_col):
        level_count = side_col.shape[0]
        row_sel = pick(up_row, side_col)
        eye = jnp.broadcast_to(jnp.eye(rank_width, dtype=jnp.float32), row_sel.shape)
        prefix = row_sel
        shift = 1
        while shift < level_count:
            earlier = jnp.concatenate([eye[:shift], prefix[:-shift]], axis=0)
            prefix = apply_down(earlier, prefix)
            shift *= 2
        before = jnp.concatenate([eye[:1], prefix[:-1]], axis=0)
        weights = apply_down(before, pick(up_cpl, side_col))
        return weights.transpose(1, 0, 2).reshape(rank_width, level_count * rank_width)

    def climb_tree(root_coeff, stages, results):
        sides = climb_sides()
        side_col = jnp.stack([side for _, _, side in sides])
        own_first = jnp.concatenate([pick(up_col, side_col), pick(up_col, 1 - side_col)], axis=1)
        current = root_coeff
        siblings = []
        for level, (name, bit_num, _) in enumerate(sides):
            sibling = from_partner(current, name, bit_num)
            if level < len(stages):
                key, stage = stages[level]
                sibling, results[key] = lax.optimization_barrier((sibling, stage()))
            siblings.append(sibling)
            if level + 1 < len(sides):
                stacked = jnp.concatenate([current, sibling], axis=0)
                current = apply_up(own_first[level], stacked)
        stacked = jnp.concatenate(siblings, axis=0)
        return apply_down(field_weights(side_col), stacked)

    def apply_image(vectors):
        columns = vectors.shape[0]
        ordered = jnp.take(vectors, order_row, axis=1).astype(jnp.bfloat16)
        leaf_blocks = ordered.reshape(columns, leaves_dev, leaf_size)
        leaf_coeff = jnp.einsum(
            "clp,lpk->lkc", leaf_blocks, col_basis, preferred_element_type=jnp.float32
        )
        leaf_round = leaf_coeff.astype(jnp.bfloat16)
        current = leaf_coeff
        offsets = []
        start_at = 0
        while current.shape[0] > 1:
            node_count = current.shape[0]
            moved_up = apply_up(col_local[start_at : start_at + node_count], current)
            paired = moved_up.reshape(node_count // 2, 2, rank_width, columns)
            current = paired[:, 0] + paired[:, 1]
            offsets.append(start_at)
            start_at = start_at + node_count
        width_all = 3 * leaves_dev
        results = {}

        def leaf_paths():
            paths = None
            for start_at in reversed(offsets):
                node_count = 2 if paths is None else paths.shape[0] * 2
                rows = row_local[start_at : start_at + node_count]
                paths = rows if paths is None else apply_down(rows, jnp.repeat(paths, 2, axis=0))
            return paths

        def near_square():
            return near_blocks.reshape(leaves_dev, near_blocks.shape[1], leaf_size, leaf_size)

        def far_square():
            return far_blocks.reshape(leaves_dev, far_blocks.shape[1], rank_width, rank_width)

        def far_picked():
            coeff_window = extended(results["win_in"][1], SUB_AXES, 0)
            return coeff_window[jnp.minimum(far_index, width_all - 1)]

        def far_sum():
            far_weight = jnp.where(far_index < width_all, far_scale, jnp.zeros_like(far_scale))
            scaled = results["far_pick"].astype(jnp.float32) * far_weight[:, :, None, None]
            return jnp.einsum("lkab,lkbc->lac", results["far_sq"], scaled, precision=best_precision)

        def near_picked():
            x_window = extended(results["win_in"][0], SUB_AXES, 1)
            return x_window[:, jnp.minimum(near_index, width_all - 1)]

        def near_total():
            near_weight = jnp.where(near_index < width_all, near_scale, jnp.zeros_like(near_scale))
            scaled = results["near_pick"].astype(jnp.float32) * near_weight[None, :, :, None]
            return jnp.einsum("lkpq,clkq->clp", results["near_sq"], scaled, precision=best_precision)

        stages = [
            ("win_in", lambda: (leaf_blocks, leaf_round)),
            ("near_sq", near_square),
            ("far_sq", far_square),
            ("far_pick", far_picked),
            ("far_sum", far_sum),
            ("near_pick", near_picked),
            ("near_sum", near_total),
            ("paths", leaf_paths),
        ]
        root_field = climb_tree(current[0], stages, results)
        for key, stage in stages:
            if key not in results:
                results[key] = stage()
        paths = results["paths"]
        near_sum = results["near_sum"]
        local_field = apply_down(paths, jnp.broadcast_to(root_field, (leaves_dev,) + root_field.shape))
        leaf_field = local_field + results["far_sum"]
        field_round = leaf_field.astype(jnp.bfloat16)
        far_out = jnp.einsum(
            "lpk,lkc->clp", row_basis, field_round, preferred_element_type=jnp.float32
        )
        image = (far_out + near_sum).reshape(columns, leaves_dev * leaf_size)
        return jnp.zeros_like(image).at[:, order_row].set(image)

    rhs = p_dirs.shape[0]
    both = apply_image(jnp.concatenate([p_dirs, resid], axis=0))
    return (both[:rhs], both[rhs:])


def split_mesh(mesh):
    grid = mesh.devices
    n_leaf, n_sub = grid.shape
    n_x = len({dev.coords[0] for dev in grid[:, 0]})
    n_z = len({dev.coords[2] for dev in grid[0, :]})
    cube = grid.reshape(n_x, n_leaf // n_x, n_z, n_sub // n_z)
    return jax.sharding.Mesh(cube, LEAF_AXES + SUB_AXES)


def solution(mesh):
    flat = LEAF_AXES + SUB_AXES
    rows = P(flat, None)
    return jax.shard_map(
        shards,
        mesh=split_mesh(mesh),
        in_specs=(
            P(None, flat),
            P(None, flat),
            rows,
            P(flat, None, None),
            P(flat, None, None),
            P(flat, None, None),
            rows,
            rows,
            P(flat, None, None),
            rows,
            rows,
            P(flat, None, None, None),
            P(flat, None, None, None),
            P(),
            P(),
            P(),
        ),
        out_specs=(P(None, flat), P(None, flat)),
        check_vma=False,
    )
```

```python
import jax
import jax.numpy as jnp
from jax import lax
from jax.sharding import PartitionSpec as P

best_precision = lax.Precision.HIGHEST
LEAF_AXES = ("lx", "ly")
SUB_AXES = ("lz", "lc")
CLIMB_AXES = ("lc", "lz", "ly", "lx")


def from_partner(value, axis, distance):
    mask = 2**distance
    pairs = [(source, source ^ mask) for source in range(lax.axis_size(axis))]
    return lax.ppermute(value, axis, pairs)


def extended(block, axis, dim):
    count = 1
    for name in axis:
        count = count * lax.axis_size(name)
    forward = [(i, i + 1) for i in range(count - 1)]
    backward = [(target, source) for source, target in forward]
    low = lax.ppermute(block, axis, forward)
    high = lax.ppermute(block, axis, backward)
    return jnp.concatenate([low, block, high], axis=dim)


def apply_up(matrix, coeffs):
    return jnp.einsum("...ab,...ac->...bc", matrix, coeffs, precision=best_precision)


def apply_down(matrix, coeffs):
    return jnp.einsum("...ab,...bc->...ac", matrix, coeffs, precision=best_precision)


def shards(
    p_dirs,
    resid,
    perm,
    col_basis,
    row_basis,
    near_blocks,
    near_scale,
    near_index,
    far_blocks,
    far_scale,
    far_index,
    loc_col,
    loc_row,
    up_col,
    up_row,
    up_cpl,
):
    leaves_dev, leaf_size, rank_width = col_basis.shape
    order_row = perm[0]
    col_local = loc_col[0].astype(jnp.float32)
    row_local = loc_row[0].astype(jnp.float32)

    def climb_sides():
        sides = []
        for name in CLIMB_AXES:
            for bit_num in range(lax.axis_size(name).bit_length() - 1):
                sides.append((name, bit_num, lax.axis_index(name) >> bit_num & 1))
        return sides

    def pick(table, side_col):
        return jnp.where(side_col[:, None, None] == 1, table[1][None], table[0][None])

    def field_weights(side_col):
        level_count = side_col.shape[0]
        row_sel = pick(up_row, side_col)
        eye = jnp.broadcast_to(jnp.eye(rank_width, dtype=jnp.float32), row_sel.shape)
        prefix = row_sel
        shift = 1
        while shift < level_count:
            earlier = jnp.concatenate([eye[:shift], prefix[:-shift]], axis=0)
            prefix = apply_down(earlier, prefix)
            shift *= 2
        before = jnp.concatenate([eye[:1], prefix[:-1]], axis=0)
        weights = apply_down(before, pick(up_cpl, side_col))
        return weights.transpose(1, 0, 2).reshape(rank_width, level_count * rank_width)

    def climb_tree(root_coeff, stages, results):
        sides = climb_sides()
        side_col = jnp.stack([side for _, _, side in sides])
        own_first = jnp.concatenate([pick(up_col, side_col), pick(up_col, 1 - side_col)], axis=1)
        current = root_coeff
        siblings = []
        for level, (name, bit_num, _) in enumerate(sides):
            sibling = from_partner(current, name, bit_num)
            if level < len(stages):
                key, stage = stages[level]
                sibling, results[key] = lax.optimization_barrier((sibling, stage()))
            siblings.append(sibling)
            if level + 1 < len(sides):
                stacked = jnp.concatenate([current, sibling], axis=0)
                current = apply_up(own_first[level], stacked)
        stacked = jnp.concatenate(siblings, axis=0)
        return apply_down(field_weights(side_col), stacked)

    def apply_image(vectors):
        columns = vectors.shape[0]
        ordered = jnp.take(vectors, order_row, axis=1).astype(jnp.bfloat16)
        leaf_blocks = ordered.reshape(columns, leaves_dev, leaf_size)
        leaf_coeff = jnp.einsum(
            "clp,lpk->lkc", leaf_blocks, col_basis, preferred_element_type=jnp.float32
        )
        leaf_round = leaf_coeff.astype(jnp.bfloat16)
        current = leaf_coeff
        offsets = []
        start_at = 0
        while current.shape[0] > 1:
            node_count = current.shape[0]
            moved_up = apply_up(col_local[start_at : start_at + node_count], current)
            paired = moved_up.reshape(node_count // 2, 2, rank_width, columns)
            current = paired[:, 0] + paired[:, 1]
            offsets.append(start_at)
            start_at = start_at + node_count
        width_all = 3 * leaves_dev
        results = {}

        def leaf_paths():
            paths = None
            for start_at in reversed(offsets):
                node_count = 2 if paths is None else paths.shape[0] * 2
                rows = row_local[start_at : start_at + node_count]
                paths = rows if paths is None else apply_down(rows, jnp.repeat(paths, 2, axis=0))
            return paths

        def near_square():
            return near_blocks.reshape(leaves_dev, near_blocks.shape[1], leaf_size, leaf_size)

        def far_square():
            return far_blocks.reshape(leaves_dev, far_blocks.shape[1], rank_width, rank_width)

        def far_picked():
            coeff_window = extended(results["win_in"][1], SUB_AXES, 0)
            return coeff_window[jnp.minimum(far_index, width_all - 1)]

        def far_sum():
            far_weight = jnp.where(far_index < width_all, far_scale, jnp.zeros_like(far_scale))
            scaled = results["far_pick"].astype(jnp.float32) * far_weight[:, :, None, None]
            return jnp.einsum("lkab,lkbc->lac", results["far_sq"], scaled, precision=best_precision)

        def near_picked():
            x_window = extended(results["win_in"][0], SUB_AXES, 1)
            return x_window[:, jnp.minimum(near_index, width_all - 1)]

        def near_total():
            near_weight = jnp.where(near_index < width_all, near_scale, jnp.zeros_like(near_scale))
            scaled = results["near_pick"].astype(jnp.float32) * near_weight[None, :, :, None]
            return jnp.einsum("lkpq,clkq->clp", results["near_sq"], scaled, precision=best_precision)

        stages = [
            ("near_sq", near_square),
            ("far_sq", far_square),
            ("paths", leaf_paths),
            ("win_in", lambda: (leaf_blocks, leaf_round)),
            ("spare", lambda: jnp.zeros((), jnp.float32)),
            ("far_pick", far_picked),
            ("far_sum", far_sum),
            ("near_pick", near_picked),
            ("near_sum", near_total),
        ]
        root_field = climb_tree(current[0], stages, results)
        for key, stage in stages:
            if key not in results:
                results[key] = stage()
        paths = results["paths"]
        near_sum = results["near_sum"]
        local_field = apply_down(paths, jnp.broadcast_to(root_field, (leaves_dev,) + root_field.shape))
        leaf_field = local_field + results["far_sum"]
        field_round = leaf_field.astype(jnp.bfloat16)
        far_out = jnp.einsum(
            "lpk,lkc->clp", row_basis, field_round, preferred_element_type=jnp.float32
        )
        image = (far_out + near_sum).reshape(columns, leaves_dev * leaf_size)
        return jnp.zeros_like(image).at[:, order_row].set(image)

    rhs = p_dirs.shape[0]
    both = apply_image(jnp.concatenate([p_dirs, resid], axis=0))
    return (both[:rhs], both[rhs:])


def split_mesh(mesh):
    grid = mesh.devices
    n_leaf, n_sub = grid.shape
    n_x = len({dev.coords[0] for dev in grid[:, 0]})
    n_z = len({dev.coords[2] for dev in grid[0, :]})
    cube = grid.reshape(n_x, n_leaf // n_x, n_z, n_sub // n_z)
    return jax.sharding.Mesh(cube, LEAF_AXES + SUB_AXES)


def solution(mesh):
    flat = LEAF_AXES + SUB_AXES
    rows = P(flat, None)
    return jax.shard_map(
        shards,
        mesh=split_mesh(mesh),
        in_specs=(
            P(None, flat),
            P(None, flat),
            rows,
            P(flat, None, None),
            P(flat, None, None),
            P(flat, None, None),
            rows,
            rows,
            P(flat, None, None),
            rows,
            rows,
            P(flat, None, None, None),
            P(flat, None, None, None),
            P(),
            P(),
            P(),
        ),
        out_specs=(P(None, flat), P(None, flat)),
        check_vma=False,
    )
```

```python
import jax
import jax.numpy as jnp
from jax import lax
from jax.sharding import PartitionSpec as P

best_precision = lax.Precision.HIGHEST
LEAF_AXES = ("lx", "ly")
SUB_AXES = ("lz", "lc")
CLIMB_AXES = ("lc", "lz", "ly", "lx")


def from_partner(value, axis, distance):
    mask = 2**distance
    pairs = [(source, source ^ mask) for source in range(lax.axis_size(axis))]
    return lax.ppermute(value, axis, pairs)


def extended(block, axis, dim):
    count = 1
    for name in axis:
        count = count * lax.axis_size(name)
    forward = [(i, i + 1) for i in range(count - 1)]
    backward = [(target, source) for source, target in forward]
    low = lax.ppermute(block, axis, forward)
    high = lax.ppermute(block, axis, backward)
    return jnp.concatenate([low, block, high], axis=dim)


def apply_up(matrix, coeffs):
    return jnp.einsum("...ab,...ac->...bc", matrix, coeffs, precision=best_precision)


def apply_down(matrix, coeffs):
    return jnp.einsum("...ab,...bc->...ac", matrix, coeffs, precision=best_precision)


def shards(
    p_dirs,
    resid,
    perm,
    col_basis,
    row_basis,
    near_blocks,
    near_scale,
    near_index,
    far_blocks,
    far_scale,
    far_index,
    loc_col,
    loc_row,
    up_col,
    up_row,
    up_cpl,
):
    leaves_dev, leaf_size, rank_width = col_basis.shape
    order_row = perm[0]
    col_local = loc_col[0].astype(jnp.float32)
    row_local = loc_row[0].astype(jnp.float32)

    def climb_sides():
        sides = []
        for name in CLIMB_AXES:
            for bit_num in range(lax.axis_size(name).bit_length() - 1):
                sides.append((name, bit_num, lax.axis_index(name) >> bit_num & 1))
        return sides

    def pick(table, side_col):
        return jnp.where(side_col[:, None, None] == 1, table[1][None], table[0][None])

    def field_weights(side_col):
        level_count = side_col.shape[0]
        row_sel = pick(up_row, side_col)
        eye = jnp.broadcast_to(jnp.eye(rank_width, dtype=jnp.float32), row_sel.shape)
        prefix = row_sel
        shift = 1
        while shift < level_count:
            earlier = jnp.concatenate([eye[:shift], prefix[:-shift]], axis=0)
            prefix = apply_down(earlier, prefix)
            shift *= 2
        before = jnp.concatenate([eye[:1], prefix[:-1]], axis=0)
        weights = apply_down(before, pick(up_cpl, side_col))
        return weights.transpose(1, 0, 2).reshape(rank_width, level_count * rank_width)

    def climb_tree(root_coeff, stages, results):
        sides = climb_sides()
        side_col = jnp.stack([side for _, _, side in sides])
        own_first = jnp.concatenate([pick(up_col, side_col), pick(up_col, 1 - side_col)], axis=1)
        current = root_coeff
        siblings = []
        for level, (name, bit_num, _) in enumerate(sides):
            sibling = from_partner(current, name, bit_num)
            if level < len(stages):
                key, stage = stages[level]
                sibling, results[key] = lax.optimization_barrier((sibling, stage()))
            siblings.append(sibling)
            if level + 1 < len(sides):
                stacked = jnp.concatenate([current, sibling], axis=0)
                current = apply_up(own_first[level], stacked)
        stacked = jnp.concatenate(siblings, axis=0)
        return apply_down(field_weights(side_col), stacked)

    def apply_image(vectors):
        columns = vectors.shape[0]
        ordered = jnp.take(vectors, order_row, axis=1).astype(jnp.bfloat16)
        leaf_blocks = ordered.reshape(columns, leaves_dev, leaf_size)
        leaf_coeff = jnp.einsum(
            "clp,lpk->lkc", leaf_blocks, col_basis, preferred_element_type=jnp.float32
        )
        leaf_round = leaf_coeff.astype(jnp.bfloat16)
        current = leaf_coeff
        offsets = []
        start_at = 0
        while current.shape[0] > 1:
            node_count = current.shape[0]
            moved_up = apply_up(col_local[start_at : start_at + node_count], current)
            paired = moved_up.reshape(node_count // 2, 2, rank_width, columns)
            current = paired[:, 0] + paired[:, 1]
            offsets.append(start_at)
            start_at = start_at + node_count
        width_all = 3 * leaves_dev
        results = {}

        def leaf_paths():
            paths = None
            for start_at in reversed(offsets):
                node_count = 2 if paths is None else paths.shape[0] * 2
                rows = row_local[start_at : start_at + node_count]
                paths = rows if paths is None else apply_down(rows, jnp.repeat(paths, 2, axis=0))
            return paths

        def near_square():
            return near_blocks.reshape(leaves_dev, near_blocks.shape[1], leaf_size, leaf_size)

        def far_square():
            return far_blocks.reshape(leaves_dev, far_blocks.shape[1], rank_width, rank_width)

        def far_picked():
            coeff_window = extended(results["win_in"][1], SUB_AXES, 0)
            return coeff_window[jnp.minimum(far_index, width_all - 1)]

        def far_sum():
            far_weight = jnp.where(far_index < width_all, far_scale, jnp.zeros_like(far_scale))
            scaled = results["far_pick"].astype(jnp.float32) * far_weight[:, :, None, None]
            return jnp.einsum("lkab,lkbc->lac", results["far_sq"], scaled, precision=best_precision)

        def near_picked():
            x_window = extended(results["win_in"][0], SUB_AXES, 1)
            return x_window[:, jnp.minimum(near_index, width_all - 1)]

        def near_total():
            near_weight = jnp.where(near_index < width_all, near_scale, jnp.zeros_like(near_scale))
            scaled = results["near_pick"].astype(jnp.float32) * near_weight[None, :, :, None]
            return jnp.einsum("lkpq,clkq->clp", results["near_sq"], scaled, precision=best_precision)

        stages = [
            ("paths", leaf_paths),
            ("spare_a", lambda: jnp.zeros((), jnp.float32)),
            ("far_sq", far_square),
            ("near_sq", near_square),
            ("win_in", lambda: (leaf_blocks, leaf_round)),
            ("spare_b", lambda: jnp.zeros((), jnp.float32)),
            ("far_pick", far_picked),
            ("far_sum", far_sum),
            ("near_pick", near_picked),
            ("near_sum", near_total),
        ]
        root_field = climb_tree(current[0], stages, results)
        for key, stage in stages:
            if key not in results:
                results[key] = stage()
        paths = results["paths"]
        near_sum = results["near_sum"]
        local_field = apply_down(paths, jnp.broadcast_to(root_field, (leaves_dev,) + root_field.shape))
        leaf_field = local_field + results["far_sum"]
        field_round = leaf_field.astype(jnp.bfloat16)
        far_out = jnp.einsum(
            "lpk,lkc->clp", row_basis, field_round, preferred_element_type=jnp.float32
        )
        image = (far_out + near_sum).reshape(columns, leaves_dev * leaf_size)
        return jnp.zeros_like(image).at[:, order_row].set(image)

    rhs = p_dirs.shape[0]
    both = apply_image(jnp.concatenate([p_dirs, resid], axis=0))
    return (both[:rhs], both[rhs:])


def split_mesh(mesh):
    grid = mesh.devices
    n_leaf, n_sub = grid.shape
    n_x = len({dev.coords[0] for dev in grid[:, 0]})
    n_z = len({dev.coords[2] for dev in grid[0, :]})
    cube = grid.reshape(n_x, n_leaf // n_x, n_z, n_sub // n_z)
    return jax.sharding.Mesh(cube, LEAF_AXES + SUB_AXES)


def solution(mesh):
    flat = LEAF_AXES + SUB_AXES
    rows = P(flat, None)
    return jax.shard_map(
        shards,
        mesh=split_mesh(mesh),
        in_specs=(
            P(None, flat),
            P(None, flat),
            rows,
            P(flat, None, None),
            P(flat, None, None),
            P(flat, None, None),
            rows,
            rows,
            P(flat, None, None),
            rows,
            rows,
            P(flat, None, None, None),
            P(flat, None, None, None),
            P(),
            P(),
            P(),
        ),
        out_specs=(P(None, flat), P(None, flat)),
        check_vma=False,
    )
```

```python
import jax
import jax.numpy as jnp
from jax import lax
from jax.sharding import PartitionSpec as P

best_precision = lax.Precision.HIGHEST
LEAF_AXES = ("lx", "ly")
SUB_AXES = ("lz", "lc")
CLIMB_AXES = ("lc", "lz", "ly", "lx")


def from_partner(value, axis, distance):
    mask = 2**distance
    pairs = [(source, source ^ mask) for source in range(lax.axis_size(axis))]
    return lax.ppermute(value, axis, pairs)


def neighbours(block, axis):
    count = 1
    for name in axis:
        count = count * lax.axis_size(name)
    forward = [(i, i + 1) for i in range(count - 1)]
    backward = [(target, source) for source, target in forward]
    return lax.ppermute(block, axis, forward), lax.ppermute(block, axis, backward)


def extended(block, axis, dim):
    count = 1
    for name in axis:
        count = count * lax.axis_size(name)
    forward = [(i, i + 1) for i in range(count - 1)]
    backward = [(target, source) for source, target in forward]
    low = lax.ppermute(block, axis, forward)
    high = lax.ppermute(block, axis, backward)
    return jnp.concatenate([low, block, high], axis=dim)


def apply_up(matrix, coeffs):
    return jnp.einsum("...ab,...ac->...bc", matrix, coeffs, precision=best_precision)


def apply_down(matrix, coeffs):
    return jnp.einsum("...ab,...bc->...ac", matrix, coeffs, precision=best_precision)


def shards(
    p_dirs,
    resid,
    perm,
    col_basis,
    row_basis,
    near_blocks,
    near_scale,
    near_index,
    far_blocks,
    far_scale,
    far_index,
    loc_col,
    loc_row,
    up_col,
    up_row,
    up_cpl,
):
    leaves_dev, leaf_size, rank_width = col_basis.shape
    order_row = perm[0]
    col_local = loc_col[0].astype(jnp.float32)
    row_local = loc_row[0].astype(jnp.float32)

    def climb_sides():
        sides = []
        for name in CLIMB_AXES:
            for bit_num in range(lax.axis_size(name).bit_length() - 1):
                sides.append((name, bit_num, lax.axis_index(name) >> bit_num & 1))
        return sides

    def pick(table, side_col):
        return jnp.where(side_col[:, None, None] == 1, table[1][None], table[0][None])

    def field_weights(side_col):
        level_count = side_col.shape[0]
        row_sel = pick(up_row, side_col)
        eye = jnp.broadcast_to(jnp.eye(rank_width, dtype=jnp.float32), row_sel.shape)
        prefix = row_sel
        shift = 1
        while shift < level_count:
            earlier = jnp.concatenate([eye[:shift], prefix[:-shift]], axis=0)
            prefix = apply_down(earlier, prefix)
            shift *= 2
        before = jnp.concatenate([eye[:1], prefix[:-1]], axis=0)
        weights = apply_down(before, pick(up_cpl, side_col))
        return weights.transpose(1, 0, 2).reshape(rank_width, level_count * rank_width)

    def climb_tree(root_coeff, stages, results):
        sides = climb_sides()
        side_col = jnp.stack([side for _, _, side in sides])
        own_first = jnp.concatenate([pick(up_col, side_col), pick(up_col, 1 - side_col)], axis=1)
        current = root_coeff
        siblings = []
        for level, (name, bit_num, _) in enumerate(sides):
            sibling = from_partner(current, name, bit_num)
            if level < len(stages):
                key, stage = stages[level]
                sibling, results[key] = lax.optimization_barrier((sibling, stage()))
            siblings.append(sibling)
            if level + 1 < len(sides):
                stacked = jnp.concatenate([current, sibling], axis=0)
                current = apply_up(own_first[level], stacked)
        stacked = jnp.concatenate(siblings, axis=0)
        return apply_down(field_weights(side_col), stacked)

    def apply_image(vectors):
        columns = vectors.shape[0]
        ordered = jnp.take(vectors, order_row, axis=1).astype(jnp.bfloat16)
        leaf_blocks = ordered.reshape(columns, leaves_dev, leaf_size)
        leaf_coeff = jnp.einsum(
            "clp,lpk->lkc", leaf_blocks, col_basis, preferred_element_type=jnp.float32
        )
        leaf_round = leaf_coeff.astype(jnp.bfloat16)
        current = leaf_coeff
        offsets = []
        start_at = 0
        while current.shape[0] > 1:
            node_count = current.shape[0]
            moved_up = apply_up(col_local[start_at : start_at + node_count], current)
            paired = moved_up.reshape(node_count // 2, 2, rank_width, columns)
            current = paired[:, 0] + paired[:, 1]
            offsets.append(start_at)
            start_at = start_at + node_count
        width_all = 3 * leaves_dev
        results = {}

        def leaf_paths():
            paths = None
            for start_at in reversed(offsets):
                node_count = 2 if paths is None else paths.shape[0] * 2
                rows = row_local[start_at : start_at + node_count]
                paths = rows if paths is None else apply_down(rows, jnp.repeat(paths, 2, axis=0))
            return paths

        def near_square():
            return near_blocks.reshape(leaves_dev, near_blocks.shape[1], leaf_size, leaf_size)

        def far_square():
            return far_blocks.reshape(leaves_dev, far_blocks.shape[1], rank_width, rank_width)

        windows = {}

        def window_pair():
            if not windows:
                blocks, coeffs = results["win_in"]
                columns_x, leaf_count, points = blocks.shape
                coeff_leaves, coeff_rank, coeff_cols = coeffs.shape
                if coeff_rank == leaf_count and coeff_cols <= points:
                    padded = jnp.pad(coeffs, ((0, 0), (0, 0), (0, points - coeff_cols)))
                    packed = jnp.concatenate([blocks, padded], axis=0)
                    low, high = neighbours(packed, SUB_AXES)
                    windows["x"] = jnp.concatenate(
                        [low[:columns_x], blocks, high[:columns_x]], axis=1
                    )
                    windows["c"] = jnp.concatenate(
                        [low[columns_x:, :, :coeff_cols], coeffs, high[columns_x:, :, :coeff_cols]],
                        axis=0,
                    )
                else:
                    windows["x"] = extended(blocks, SUB_AXES, 1)
                    windows["c"] = extended(coeffs, SUB_AXES, 0)
            return windows["x"], windows["c"]

        def far_picked():
            coeff_window = window_pair()[1]
            return coeff_window[jnp.minimum(far_index, width_all - 1)]

        def far_sum():
            far_weight = jnp.where(far_index < width_all, far_scale, jnp.zeros_like(far_scale))
            scaled = results["far_pick"].astype(jnp.float32) * far_weight[:, :, None, None]
            return jnp.einsum("lkab,lkbc->lac", results["far_sq"], scaled, precision=best_precision)

        def near_picked():
            x_window = window_pair()[0]
            return x_window[:, jnp.minimum(near_index, width_all - 1)]

        def near_total():
            near_weight = jnp.where(near_index < width_all, near_scale, jnp.zeros_like(near_scale))
            scaled = results["near_pick"].astype(jnp.float32) * near_weight[None, :, :, None]
            return jnp.einsum("lkpq,clkq->clp", results["near_sq"], scaled, precision=best_precision)

        stages = [
            ("paths", leaf_paths),
            ("spare_a", lambda: jnp.zeros((), jnp.float32)),
            ("far_sq", far_square),
            ("near_sq", near_square),
            ("win_in", lambda: (leaf_blocks, leaf_round)),
            ("spare_b", lambda: jnp.zeros((), jnp.float32)),
            ("far_pick", far_picked),
            ("far_sum", far_sum),
            ("near_pick", near_picked),
            ("near_sum", near_total),
        ]
        root_field = climb_tree(current[0], stages, results)
        for key, stage in stages:
            if key not in results:
                results[key] = stage()
        paths = results["paths"]
        near_sum = results["near_sum"]
        local_field = apply_down(paths, jnp.broadcast_to(root_field, (leaves_dev,) + root_field.shape))
        leaf_field = local_field + results["far_sum"]
        field_round = leaf_field.astype(jnp.bfloat16)
        far_out = jnp.einsum(
            "lpk,lkc->clp", row_basis, field_round, preferred_element_type=jnp.float32
        )
        image = (far_out + near_sum).reshape(columns, leaves_dev * leaf_size)
        return jnp.zeros_like(image).at[:, order_row].set(image)

    rhs = p_dirs.shape[0]
    both = apply_image(jnp.concatenate([p_dirs, resid], axis=0))
    return (both[:rhs], both[rhs:])


def split_mesh(mesh):
    grid = mesh.devices
    n_leaf, n_sub = grid.shape
    n_x = len({dev.coords[0] for dev in grid[:, 0]})
    n_z = len({dev.coords[2] for dev in grid[0, :]})
    cube = grid.reshape(n_x, n_leaf // n_x, n_z, n_sub // n_z)
    return jax.sharding.Mesh(cube, LEAF_AXES + SUB_AXES)


def solution(mesh):
    flat = LEAF_AXES + SUB_AXES
    rows = P(flat, None)
    return jax.shard_map(
        shards,
        mesh=split_mesh(mesh),
        in_specs=(
            P(None, flat),
            P(None, flat),
            rows,
            P(flat, None, None),
            P(flat, None, None),
            P(flat, None, None),
            rows,
            rows,
            P(flat, None, None),
            rows,
            rows,
            P(flat, None, None, None),
            P(flat, None, None, None),
            P(),
            P(),
            P(),
        ),
        out_specs=(P(None, flat), P(None, flat)),
        check_vma=False,
    )
```

```python
import jax
import jax.numpy as jnp
from jax import lax
from jax.sharding import PartitionSpec as P

best_precision = lax.Precision.HIGHEST
LEAF_AXES = ("lx", "ly")
SUB_AXES = ("lz", "lc")
CLIMB_AXES = ("lc", "lz", "ly", "lx")


def from_partner(value, axis, distance):
    mask = 2**distance
    pairs = [(source, source ^ mask) for source in range(lax.axis_size(axis))]
    return lax.ppermute(value, axis, pairs)


def extended(block, axis, dim):
    count = 1
    for name in axis:
        count = count * lax.axis_size(name)
    forward = [(i, i + 1) for i in range(count - 1)]
    backward = [(target, source) for source, target in forward]
    low = lax.ppermute(block, axis, forward)
    high = lax.ppermute(block, axis, backward)
    return jnp.concatenate([low, block, high], axis=dim)


def apply_up(matrix, coeffs):
    return jnp.einsum("...ab,...ac->...bc", matrix, coeffs, precision=best_precision)


def apply_down(matrix, coeffs):
    return jnp.einsum("...ab,...bc->...ac", matrix, coeffs, precision=best_precision)


def shards(
    p_dirs,
    resid,
    perm,
    col_basis,
    row_basis,
    near_blocks,
    near_scale,
    near_index,
    far_blocks,
    far_scale,
    far_index,
    loc_col,
    loc_row,
    up_col,
    up_row,
    up_cpl,
):
    leaves_dev, leaf_size, rank_width = col_basis.shape
    order_row = perm[0]
    col_local = loc_col[0].astype(jnp.float32)
    row_local = loc_row[0].astype(jnp.float32)

    def climb_sides():
        sides = []
        for name in CLIMB_AXES:
            for bit_num in range(lax.axis_size(name).bit_length() - 1):
                sides.append((name, bit_num, lax.axis_index(name) >> bit_num & 1))
        return sides

    def pick(table, side_col):
        return jnp.where(side_col[:, None, None] == 1, table[1][None], table[0][None])

    def field_weights(side_col):
        level_count = side_col.shape[0]
        row_sel = pick(up_row, side_col)
        eye = jnp.broadcast_to(jnp.eye(rank_width, dtype=jnp.float32), row_sel.shape)
        prefix = row_sel
        shift = 1
        while shift < level_count:
            earlier = jnp.concatenate([eye[:shift], prefix[:-shift]], axis=0)
            prefix = apply_down(earlier, prefix)
            shift *= 2
        before = jnp.concatenate([eye[:1], prefix[:-1]], axis=0)
        weights = apply_down(before, pick(up_cpl, side_col))
        return weights.transpose(1, 0, 2).reshape(rank_width, level_count * rank_width)

    def climb_tree(root_coeff, stages, results):
        sides = climb_sides()
        side_col = jnp.stack([side for _, _, side in sides])
        own_first = jnp.concatenate([pick(up_col, side_col), pick(up_col, 1 - side_col)], axis=1)
        current = root_coeff
        siblings = []
        for level, (name, bit_num, _) in enumerate(sides):
            sibling = from_partner(current, name, bit_num)
            if level < len(stages):
                key, stage = stages[level]
                sibling, results[key] = lax.optimization_barrier((sibling, stage()))
            siblings.append(sibling)
            if level + 1 < len(sides):
                stacked = jnp.concatenate([current, sibling], axis=0)
                current = apply_up(own_first[level], stacked)
        stacked = jnp.concatenate(siblings, axis=0)
        return apply_down(field_weights(side_col), stacked)

    def apply_image(vectors):
        columns = vectors.shape[0]
        ordered = jnp.take(vectors, order_row, axis=1).astype(jnp.bfloat16)
        leaf_blocks = ordered.reshape(columns, leaves_dev, leaf_size)
        leaf_coeff = jnp.einsum(
            "clp,lpk->lkc", leaf_blocks, col_basis, preferred_element_type=jnp.float32
        )
        leaf_round = leaf_coeff.astype(jnp.bfloat16)
        current = leaf_coeff
        offsets = []
        start_at = 0
        while current.shape[0] > 1:
            node_count = current.shape[0]
            moved_up = apply_up(col_local[start_at : start_at + node_count], current)
            paired = moved_up.reshape(node_count // 2, 2, rank_width, columns)
            current = paired[:, 0] + paired[:, 1]
            offsets.append(start_at)
            start_at = start_at + node_count
        width_all = 3 * leaves_dev
        results = {}

        def leaf_paths():
            paths = None
            for start_at in reversed(offsets):
                node_count = 2 if paths is None else paths.shape[0] * 2
                rows = row_local[start_at : start_at + node_count]
                paths = rows if paths is None else apply_down(rows, jnp.repeat(paths, 2, axis=0))
            return paths

        def near_square():
            return near_blocks.reshape(leaves_dev, near_blocks.shape[1], leaf_size, leaf_size)

        def far_square():
            return far_blocks.reshape(leaves_dev, far_blocks.shape[1], rank_width, rank_width)

        def far_picked():
            coeff_window = extended(results["win_in"][1], SUB_AXES, 0)
            return coeff_window[jnp.minimum(far_index, width_all - 1)]

        def far_sum():
            far_weight = jnp.where(far_index < width_all, far_scale, jnp.zeros_like(far_scale))
            scaled = results["far_pick"].astype(jnp.float32) * far_weight[:, :, None, None]
            return jnp.einsum("lkab,lkbc->lac", results["far_sq"], scaled, precision=best_precision)

        def near_picked():
            x_window = extended(results["win_in"][0], SUB_AXES, 1)
            return x_window[:, jnp.minimum(near_index, width_all - 1)]

        def near_total():
            near_weight = jnp.where(near_index < width_all, near_scale, jnp.zeros_like(near_scale))
            scaled = results["near_pick"].astype(jnp.float32) * near_weight[None, :, :, None]
            return jnp.einsum("lkpq,clkq->clp", results["near_sq"], scaled, precision=best_precision)

        stages = [
            ("spare_a", lambda: jnp.zeros((), jnp.float32)),
            ("paths", leaf_paths),
            ("far_sq", far_square),
            ("near_sq", near_square),
            ("win_in", lambda: (leaf_blocks, leaf_round)),
            ("spare_b", lambda: jnp.zeros((), jnp.float32)),
            ("far_pick", far_picked),
            ("far_sum", far_sum),
            ("near_pick", near_picked),
            ("near_sum", near_total),
        ]
        root_field = climb_tree(current[0], stages, results)
        for key, stage in stages:
            if key not in results:
                results[key] = stage()
        paths = results["paths"]
        near_sum = results["near_sum"]
        local_field = apply_down(paths, jnp.broadcast_to(root_field, (leaves_dev,) + root_field.shape))
        leaf_field = local_field + results["far_sum"]
        field_round = leaf_field.astype(jnp.bfloat16)
        far_out = jnp.einsum(
            "lpk,lkc->clp", row_basis, field_round, preferred_element_type=jnp.float32
        )
        image = (far_out + near_sum).reshape(columns, leaves_dev * leaf_size)
        return jnp.zeros_like(image).at[:, order_row].set(image)

    rhs = p_dirs.shape[0]
    both = apply_image(jnp.concatenate([p_dirs, resid], axis=0))
    return (both[:rhs], both[rhs:])


def split_mesh(mesh):
    grid = mesh.devices
    n_leaf, n_sub = grid.shape
    n_x = len({dev.coords[0] for dev in grid[:, 0]})
    n_z = len({dev.coords[2] for dev in grid[0, :]})
    cube = grid.reshape(n_x, n_leaf // n_x, n_z, n_sub // n_z)
    return jax.sharding.Mesh(cube, LEAF_AXES + SUB_AXES)


def solution(mesh):
    flat = LEAF_AXES + SUB_AXES
    rows = P(flat, None)
    return jax.shard_map(
        shards,
        mesh=split_mesh(mesh),
        in_specs=(
            P(None, flat),
            P(None, flat),
            rows,
            P(flat, None, None),
            P(flat, None, None),
            P(flat, None, None),
            rows,
            rows,
            P(flat, None, None),
            rows,
            rows,
            P(flat, None, None, None),
            P(flat, None, None, None),
            P(),
            P(),
            P(),
        ),
        out_specs=(P(None, flat), P(None, flat)),
        check_vma=False,
    )
```

```python
import jax
import jax.numpy as jnp
from jax import lax
from jax.sharding import PartitionSpec as P

best_precision = lax.Precision.HIGHEST
LEAF_AXES = ("lx", "ly")
SUB_AXES = ("lz", "lc")
CLIMB_AXES = ("lc", "lz", "ly", "lx")


def from_partner(value, axis, distance):
    mask = 2**distance
    pairs = [(source, source ^ mask) for source in range(lax.axis_size(axis))]
    return lax.ppermute(value, axis, pairs)


def extended(block, axis, dim):
    count = 1
    for name in axis:
        count = count * lax.axis_size(name)
    forward = [(i, i + 1) for i in range(count - 1)]
    backward = [(target, source) for source, target in forward]
    low = lax.ppermute(block, axis, forward)
    high = lax.ppermute(block, axis, backward)
    return jnp.concatenate([low, block, high], axis=dim)


def apply_up(matrix, coeffs):
    return jnp.einsum("...ab,...ac->...bc", matrix, coeffs, precision=best_precision)


def apply_down(matrix, coeffs):
    return jnp.einsum("...ab,...bc->...ac", matrix, coeffs, precision=best_precision)


def shards(
    p_dirs,
    resid,
    perm,
    col_basis,
    row_basis,
    near_blocks,
    near_scale,
    near_index,
    far_blocks,
    far_scale,
    far_index,
    loc_col,
    loc_row,
    up_col,
    up_row,
    up_cpl,
):
    leaves_dev, leaf_size, rank_width = col_basis.shape
    order_row = perm[0]
    col_local = loc_col[0].astype(jnp.float32)
    row_local = loc_row[0].astype(jnp.float32)

    def climb_sides():
        sides = []
        for name in CLIMB_AXES:
            for bit_num in range(lax.axis_size(name).bit_length() - 1):
                sides.append((name, bit_num, lax.axis_index(name) >> bit_num & 1))
        return sides

    def pick(table, side_col):
        return jnp.where(side_col[:, None, None] == 1, table[1][None], table[0][None])

    def field_weights(side_col, row_table, cpl_table):
        level_count = side_col.shape[0]
        row_sel = pick(row_table, side_col)
        eye = jnp.broadcast_to(jnp.eye(rank_width, dtype=jnp.float32), row_sel.shape)
        prefix = row_sel
        shift = 1
        while shift < level_count:
            earlier = jnp.concatenate([eye[:shift], prefix[:-shift]], axis=0)
            prefix = apply_down(earlier, prefix)
            shift *= 2
        before = jnp.concatenate([eye[:1], prefix[:-1]], axis=0)
        weights = apply_down(before, pick(cpl_table, side_col))
        return weights.transpose(1, 0, 2).reshape(rank_width, level_count * rank_width)

    def climb_tree(root_coeff, stages, results):
        sides = climb_sides()
        side_col = jnp.stack([side for _, _, side in sides])
        own_first = jnp.concatenate([pick(up_col, side_col), pick(up_col, 1 - side_col)], axis=1)
        current = root_coeff
        siblings = []
        for level, (name, bit_num, _) in enumerate(sides):
            sibling = from_partner(current, name, bit_num)
            if level < len(stages):
                key, stage = stages[level]
                sibling, results[key] = lax.optimization_barrier((sibling, stage()))
            siblings.append(sibling)
            if level + 1 < len(sides):
                stacked = jnp.concatenate([current, sibling], axis=0)
                current = apply_up(own_first[level], stacked)
        stacked = jnp.concatenate(siblings, axis=0)
        return apply_down(results["late"][1], stacked)

    def apply_image(vectors):
        columns = vectors.shape[0]
        ordered = jnp.take(vectors, order_row, axis=1).astype(jnp.bfloat16)
        leaf_blocks = ordered.reshape(columns, leaves_dev, leaf_size)
        leaf_coeff = jnp.einsum(
            "clp,lpk->lkc", leaf_blocks, col_basis, preferred_element_type=jnp.float32
        )
        leaf_round = leaf_coeff.astype(jnp.bfloat16)
        current = leaf_coeff
        offsets = []
        start_at = 0
        while current.shape[0] > 1:
            node_count = current.shape[0]
            moved_up = apply_up(col_local[start_at : start_at + node_count], current)
            paired = moved_up.reshape(node_count // 2, 2, rank_width, columns)
            current = paired[:, 0] + paired[:, 1]
            offsets.append(start_at)
            start_at = start_at + node_count
        width_all = 3 * leaves_dev
        results = {}

        def leaf_paths():
            paths = None
            for start_at in reversed(offsets):
                node_count = 2 if paths is None else paths.shape[0] * 2
                rows = row_local[start_at : start_at + node_count]
                paths = rows if paths is None else apply_down(rows, jnp.repeat(paths, 2, axis=0))
            return paths

        def near_square():
            return near_blocks.reshape(leaves_dev, near_blocks.shape[1], leaf_size, leaf_size)

        def far_square():
            return far_blocks.reshape(leaves_dev, far_blocks.shape[1], rank_width, rank_width)

        def far_picked():
            coeff_window = extended(results["win_in"][1], SUB_AXES, 0)
            return coeff_window[jnp.minimum(far_index, width_all - 1)]

        def far_sum():
            far_weight = jnp.where(far_index < width_all, far_scale, jnp.zeros_like(far_scale))
            scaled = results["far_pick"].astype(jnp.float32) * far_weight[:, :, None, None]
            return jnp.einsum("lkab,lkbc->lac", results["far_sq"], scaled, precision=best_precision)

        def near_picked():
            x_window = extended(results["win_in"][0], SUB_AXES, 1)
            return x_window[:, jnp.minimum(near_index, width_all - 1)]

        def near_total():
            near_weight = jnp.where(near_index < width_all, near_scale, jnp.zeros_like(near_scale))
            scaled = results["near_pick"].astype(jnp.float32) * near_weight[None, :, :, None]
            return jnp.einsum("lkpq,clkq->clp", results["near_sq"], scaled, precision=best_precision)

        side_col = jnp.stack([side for _, _, side in climb_sides()])
        stages = [
            ("w_in", lambda: (up_row, up_cpl)),
            ("late", lambda: (leaf_paths(), field_weights(side_col, *results["w_in"]))),
            ("far_sq", far_square),
            ("near_sq", near_square),
            ("win_in", lambda: (leaf_blocks, leaf_round)),
            ("spare_b", lambda: jnp.zeros((), jnp.float32)),
            ("far_pick", far_picked),
            ("far_sum", far_sum),
            ("near_pick", near_picked),
            ("near_sum", near_total),
        ]
        root_field = climb_tree(current[0], stages, results)
        for key, stage in stages:
            if key not in results:
                results[key] = stage()
        paths = results["late"][0]
        near_sum = results["near_sum"]
        local_field = apply_down(paths, jnp.broadcast_to(root_field, (leaves_dev,) + root_field.shape))
        leaf_field = local_field + results["far_sum"]
        field_round = leaf_field.astype(jnp.bfloat16)
        far_out = jnp.einsum(
            "lpk,lkc->clp", row_basis, field_round, preferred_element_type=jnp.float32
        )
        image = (far_out + near_sum).reshape(columns, leaves_dev * leaf_size)
        return jnp.zeros_like(image).at[:, order_row].set(image)

    rhs = p_dirs.shape[0]
    both = apply_image(jnp.concatenate([p_dirs, resid], axis=0))
    return (both[:rhs], both[rhs:])


def split_mesh(mesh):
    grid = mesh.devices
    n_leaf, n_sub = grid.shape
    n_x = len({dev.coords[0] for dev in grid[:, 0]})
    n_z = len({dev.coords[2] for dev in grid[0, :]})
    cube = grid.reshape(n_x, n_leaf // n_x, n_z, n_sub // n_z)
    return jax.sharding.Mesh(cube, LEAF_AXES + SUB_AXES)


def solution(mesh):
    flat = LEAF_AXES + SUB_AXES
    rows = P(flat, None)
    return jax.shard_map(
        shards,
        mesh=split_mesh(mesh),
        in_specs=(
            P(None, flat),
            P(None, flat),
            rows,
            P(flat, None, None),
            P(flat, None, None),
            P(flat, None, None),
            rows,
            rows,
            P(flat, None, None),
            rows,
            rows,
            P(flat, None, None, None),
            P(flat, None, None, None),
            P(),
            P(),
            P(),
        ),
        out_specs=(P(None, flat), P(None, flat)),
        check_vma=False,
    )
```

```python
import jax
import jax.numpy as jnp
from jax import lax
from jax.sharding import PartitionSpec as P

best_precision = lax.Precision.HIGHEST
LEAF_AXES = ("lx", "ly")
SUB_AXES = ("lz", "lc")
CLIMB_AXES = ("lc", "lz", "ly", "lx")


def from_partner(value, axis, distance):
    mask = 2**distance
    pairs = [(source, source ^ mask) for source in range(lax.axis_size(axis))]
    return lax.ppermute(value, axis, pairs)


def extended(block, axis, dim):
    count = 1
    for name in axis:
        count = count * lax.axis_size(name)
    forward = [(i, i + 1) for i in range(count - 1)]
    backward = [(target, source) for source, target in forward]
    low = lax.ppermute(block, axis, forward)
    high = lax.ppermute(block, axis, backward)
    return jnp.concatenate([low, block, high], axis=dim)


def apply_up(matrix, coeffs):
    return jnp.einsum("...ab,...ac->...bc", matrix, coeffs, precision=best_precision)


def apply_down(matrix, coeffs):
    return jnp.einsum("...ab,...bc->...ac", matrix, coeffs, precision=best_precision)


def shards(
    p_dirs,
    resid,
    perm,
    col_basis,
    row_basis,
    near_blocks,
    near_scale,
    near_index,
    far_blocks,
    far_scale,
    far_index,
    loc_col,
    loc_row,
    up_col,
    up_row,
    up_cpl,
):
    leaves_dev, leaf_size, rank_width = col_basis.shape
    order_row = perm[0]
    col_local = loc_col[0].astype(jnp.float32)
    row_local = loc_row[0].astype(jnp.float32)

    def climb_sides():
        sides = []
        for name in CLIMB_AXES:
            for bit_num in range(lax.axis_size(name).bit_length() - 1):
                sides.append((name, bit_num, lax.axis_index(name) >> bit_num & 1))
        return sides

    def pick(table, side_col):
        return jnp.where(side_col[:, None, None] == 1, table[1][None], table[0][None])

    def field_weights(side_col, row_table, cpl_table):
        level_count = side_col.shape[0]
        row_sel = pick(row_table, side_col)
        eye = jnp.broadcast_to(jnp.eye(rank_width, dtype=jnp.float32), row_sel.shape)
        prefix = row_sel
        shift = 1
        while shift < level_count:
            earlier = jnp.concatenate([eye[:shift], prefix[:-shift]], axis=0)
            prefix = apply_down(earlier, prefix)
            shift *= 2
        before = jnp.concatenate([eye[:1], prefix[:-1]], axis=0)
        weights = apply_down(before, pick(cpl_table, side_col))
        return weights.transpose(1, 0, 2).reshape(rank_width, level_count * rank_width)

    def climb_tree(root_coeff, stages, results):
        sides = climb_sides()
        side_col = jnp.stack([side for _, _, side in sides])
        own_first = jnp.concatenate([pick(up_col, side_col), pick(up_col, 1 - side_col)], axis=1)
        current = root_coeff
        siblings = []
        for level, (name, bit_num, _) in enumerate(sides):
            sibling = from_partner(current, name, bit_num)
            if level < len(stages):
                key, stage = stages[level]
                sibling, results[key] = lax.optimization_barrier((sibling, stage()))
            siblings.append(sibling)
            if level + 1 < len(sides):
                stacked = jnp.concatenate([current, sibling], axis=0)
                current = apply_up(own_first[level], stacked)
        stacked = jnp.concatenate(siblings, axis=0)
        return apply_down(results["late"][1], stacked)

    def apply_image(vectors):
        columns = vectors.shape[0]
        ordered = jnp.take(vectors, order_row, axis=1).astype(jnp.bfloat16)
        leaf_blocks = ordered.reshape(columns, leaves_dev, leaf_size)
        leaf_coeff = jnp.einsum(
            "clp,lpk->lkc", leaf_blocks, col_basis, preferred_element_type=jnp.float32
        )
        leaf_round = leaf_coeff.astype(jnp.bfloat16)
        current = leaf_coeff
        offsets = []
        start_at = 0
        while current.shape[0] > 1:
            node_count = current.shape[0]
            total = col_local.shape[0]
            placed = jnp.pad(current, ((start_at, total - start_at - node_count), (0, 0), (0, 0)))
            moved_up = apply_up(col_local, placed)[start_at : start_at + node_count]
            paired = moved_up.reshape(node_count // 2, 2, rank_width, columns)
            current = paired[:, 0] + paired[:, 1]
            offsets.append(start_at)
            start_at = start_at + node_count
        width_all = 3 * leaves_dev
        results = {}

        def leaf_paths():
            paths = None
            for start_at in reversed(offsets):
                node_count = 2 if paths is None else paths.shape[0] * 2
                rows = row_local[start_at : start_at + node_count]
                paths = rows if paths is None else apply_down(rows, jnp.repeat(paths, 2, axis=0))
            return paths

        def near_square():
            return near_blocks.reshape(leaves_dev, near_blocks.shape[1], leaf_size, leaf_size)

        def far_square():
            return far_blocks.reshape(leaves_dev, far_blocks.shape[1], rank_width, rank_width)

        def far_picked():
            coeff_window = extended(results["win_in"][1], SUB_AXES, 0)
            return coeff_window[jnp.minimum(far_index, width_all - 1)]

        def far_sum():
            far_weight = jnp.where(far_index < width_all, far_scale, jnp.zeros_like(far_scale))
            scaled = results["far_pick"].astype(jnp.float32) * far_weight[:, :, None, None]
            return jnp.einsum("lkab,lkbc->lac", results["far_sq"], scaled, precision=best_precision)

        def near_picked():
            x_window = extended(results["win_in"][0], SUB_AXES, 1)
            return x_window[:, jnp.minimum(near_index, width_all - 1)]

        def near_total():
            near_weight = jnp.where(near_index < width_all, near_scale, jnp.zeros_like(near_scale))
            scaled = results["near_pick"].astype(jnp.float32) * near_weight[None, :, :, None]
            return jnp.einsum("lkpq,clkq->clp", results["near_sq"], scaled, precision=best_precision)

        side_col = jnp.stack([side for _, _, side in climb_sides()])
        stages = [
            ("w_in", lambda: (up_row, up_cpl)),
            ("late", lambda: (leaf_paths(), field_weights(side_col, *results["w_in"]))),
            ("far_sq", far_square),
            ("near_sq", near_square),
            ("win_in", lambda: (leaf_blocks, leaf_round)),
            ("spare_b", lambda: jnp.zeros((), jnp.float32)),
            ("far_pick", far_picked),
            ("far_sum", far_sum),
            ("near_pick", near_picked),
            ("near_sum", near_total),
        ]
        root_field = climb_tree(current[0], stages, results)
        for key, stage in stages:
            if key not in results:
                results[key] = stage()
        paths = results["late"][0]
        near_sum = results["near_sum"]
        local_field = apply_down(paths, jnp.broadcast_to(root_field, (leaves_dev,) + root_field.shape))
        leaf_field = local_field + results["far_sum"]
        field_round = leaf_field.astype(jnp.bfloat16)
        far_out = jnp.einsum(
            "lpk,lkc->clp", row_basis, field_round, preferred_element_type=jnp.float32
        )
        image = (far_out + near_sum).reshape(columns, leaves_dev * leaf_size)
        return jnp.zeros_like(image).at[:, order_row].set(image)

    rhs = p_dirs.shape[0]
    both = apply_image(jnp.concatenate([p_dirs, resid], axis=0))
    return (both[:rhs], both[rhs:])


def split_mesh(mesh):
    grid = mesh.devices
    n_leaf, n_sub = grid.shape
    n_x = len({dev.coords[0] for dev in grid[:, 0]})
    n_z = len({dev.coords[2] for dev in grid[0, :]})
    cube = grid.reshape(n_x, n_leaf // n_x, n_z, n_sub // n_z)
    return jax.sharding.Mesh(cube, LEAF_AXES + SUB_AXES)


def solution(mesh):
    flat = LEAF_AXES + SUB_AXES
    rows = P(flat, None)
    return jax.shard_map(
        shards,
        mesh=split_mesh(mesh),
        in_specs=(
            P(None, flat),
            P(None, flat),
            rows,
            P(flat, None, None),
            P(flat, None, None),
            P(flat, None, None),
            rows,
            rows,
            P(flat, None, None),
            rows,
            rows,
            P(flat, None, None, None),
            P(flat, None, None, None),
            P(),
            P(),
            P(),
        ),
        out_specs=(P(None, flat), P(None, flat)),
        check_vma=False,
    )
```
